256 devices in a mesh: chip: 2 (over core), row: 16 (over x, y), grp: 8 (over z).
Axes of the slice: x: 4, y: 4, z: 8, core: 2. Of those that a mesh axis runs over, the one named last changes fastest.
Arguments:
- old_velocity: float32 [2, 4096, 4096], P(None, 'row', ('chip', 'grp')), may hold values from -6 to 6
- surface_stress: float32 [2, 4096, 4096], P(None, 'row', ('chip', 'grp')), may hold values from -6 to 6
- mass_term: float32 [4096, 4096], P('row', ('chip', 'grp')), may hold values from 0.2 to 2
- ocean_drag: float32 [4096, 4096], P('row', ('chip', 'grp')), may hold values from 0.1 to 1
- strength: float32 [4096, 4096], P('row', ('chip', 'grp')), may hold values from 1 to 10
- ice_mask: int32 [4096, 4096], P('row', ('chip', 'grp')), may hold values from 0 to 1, as said below
- ocean_mask: int32 [4096, 4096], P('row', ('chip', 'grp')), may hold values 0 or 1
- ice_blocks: int32 [16, 32], P(('chip', 'grp')), may hold values from 0 to 63, as said below
Outputs:
- new_velocity: float32 [2, 4096, 4096], P(None, 'row', ('chip', 'grp'))
The draws below stay inside these ranges and needn't reach their ends.
Inputs may be any that keep to these rules, and one draw needn't show every extreme that they name: `ice_blocks`: entry n of row c names block n % 4 (row-major over the blocks of 128 x 128 cells of a tile) of tile row n // 4 in tile column c. Each row lists 32 different blocks; the blocks of one tile stand together, tiles with more listed blocks first; all 4 blocks of the last tile row of every column are listed. The entry at place k of a row is owned by tile row k % 16 of that column, as its block number k // 16. `ice_mask`: ice lies only in cells of the blocks listed in ice_blocks.
All inputs are finite; a program needn't handle non-finite values. No bound on the sum of `ocean_mask` on one device may be relied on, other than what follows from the above.
Results may differ from the reference program's by a relative error of at most 0.00011.
Values sent between devices are 32-bit elements; how exact they have to be, the bound alone decides.
No kernel may reach another device: no remote copies, remote signals or barrier semaphores. Data moves between devices by JAX's collectives and lax.ppermute only.
A program may use at most 128 MiB of HBM per device.

```python
import math
import jax
import jax.numpy as jnp

BS = 128
TX = 256
TY = 256
KRYLOV = 2
CYCLES = 2
SWEEPS = 2
BLOCKS_TILE = 4
SLOTS = 2
NCOL = 16
NX = 4096
NY = 4096
N_ROW = 16


def column_plan(key, column):
    column_key = jax.random.fold_in(jax.random.fold_in(key, 7), column)
    key_tiles, key_blocks, key_order = jax.random.split(column_key, 3)
    total_blocks = N_ROW * BLOCKS_TILE
    block_ids = jnp.arange(total_blocks, dtype=jnp.int32)
    tile_of = block_ids // BLOCKS_TILE
    weights = jax.random.randint(key_tiles, (N_ROW,), 0, 4)
    weights = jnp.where(jnp.arange(N_ROW) == N_ROW - 1, 8, weights)
    noise = jax.random.randint(key_blocks, (total_blocks,), 0, 4096)
    score = (weights[tile_of] * 4096 + noise) * total_blocks + block_ids
    chosen = jnp.argsort(-score)[:N_ROW * SLOTS]
    is_icy = jnp.zeros((total_blocks,), jnp.int32).at[chosen].set(1)
    counts = jnp.sum(is_icy.reshape(N_ROW, BLOCKS_TILE), axis=1)
    tie_rank = jnp.argsort(jax.random.permutation(key_order, N_ROW)).astype(jnp.int32)
    deal_key = ((BLOCKS_TILE - counts[tile_of]) * N_ROW + tie_rank[tile_of]) * BLOCKS_TILE + block_ids % BLOCKS_TILE
    deal_key = deal_key + (1 - is_icy) * (BLOCKS_TILE + 1) * N_ROW * BLOCKS_TILE
    dealt = jnp.argsort(deal_key)[:N_ROW * SLOTS].astype(jnp.int32)
    return (dealt, is_icy)


def draw_ice_blocks(key, part):
    lists, flags = jax.vmap(lambda column: column_plan(key, column))(jnp.arange(NCOL, dtype=jnp.int32))
    return lists.astype(jnp.int32)


def draw_ice_mask(key, part):
    lists, flags = jax.vmap(lambda column: column_plan(key, column))(jnp.arange(NCOL, dtype=jnp.int32))
    shaped = flags.reshape(NCOL, N_ROW, TX // BS, TY // BS)
    shaped = jnp.repeat(jnp.repeat(shaped, BS, axis=2), BS, axis=3)
    cells = shaped.transpose(1, 2, 0, 3).reshape(NX, NY)
    random_bits = jax.random.randint(jax.random.fold_in(key, 9), (NX, NY), 0, 8)
    return jnp.where(random_bits > 0, cells, 0).astype(jnp.int32)


def plant(values, key, least, high):
    longest = values.shape.index(max(values.shape))
    spots = []
    for shift in (0, 1):
        where = [jax.random.randint(jax.random.fold_in(key, axis), (), 0, length) for axis, length in enumerate(values.shape)]
        where[longest] = (where[longest] + shift) % values.shape[longest]
        spots.append(tuple(where))
    return values.at[spots[0]].set(least).at[spots[1]].set(high)


def block_scale(own_key, shape, cuts, smallest, largest):
    factor_of, own = 1.0, jax.random.fold_in(own_key, 6)
    for position, shards_of in cuts:
        heights = jnp.exp(jax.random.uniform(jax.random.fold_in(own, position), (shards_of,), jnp.float32, smallest / len(cuts), largest / len(cuts)))
        factor_of = factor_of * jnp.repeat(heights, shape[position] // shards_of).reshape([-1 if axis == position else 1 for axis in range(len(shape))])
    return factor_of


def gaussian(own_key, extent, scale, most, cuts=(), kind=jnp.bfloat16):
    drawn = scale * jax.random.normal(own_key, extent, jnp.float32)
    if cuts:
        drawn = drawn * block_scale(own_key, extent, cuts, -0.22, 0.18)
    return jnp.clip(drawn, -most, most).astype(kind)


def setup_inputs(seed: int = 0) -> dict:
    seeds = jax.random.split(jax.random.key(seed), 9)
    return {
        "old_velocity": gaussian(seeds[0], (2, NX, NY), 1.0, 6.0, ((1, 16), (2, 16)), jnp.float32),
        "surface_stress": gaussian(seeds[1], (2, NX, NY), 1.0, 6.0, ((1, 16), (2, 16)), jnp.float32),
        "mass_term": jnp.clip(jnp.exp(math.log(2.0) - 2.3025851 * jax.random.uniform(seeds[2], (NX, NY), jnp.float32) ** block_scale(seeds[2], (NX, NY), ((0, 16), (1, 16)), -0.2, 0.2)), 0.2, 2.0),
        "ocean_drag": jnp.clip(jnp.exp(math.log(1.0) - 2.3025851 * jax.random.uniform(seeds[3], (NX, NY), jnp.float32) ** block_scale(seeds[3], (NX, NY), ((0, 16), (1, 16)), -0.2, 0.2)), 0.1, 1.0),
        "strength": jnp.clip(jnp.exp(math.log(10.0) - 2.3025851 * jax.random.uniform(seeds[4], (NX, NY), jnp.float32) ** block_scale(seeds[4], (NX, NY), ((0, 16), (1, 16)), -0.2, 0.2)), 1.0, 10.0),
        "ice_mask": draw_ice_mask(jax.random.fold_in(seeds[8], 71), 0),
        "ocean_mask": plant((jax.random.randint(seeds[6], (NX, NY), 0, 10) < 9).astype(jnp.int32), jax.random.fold_in(seeds[6], 1), 0, 1),
        "ice_blocks": draw_ice_blocks(jax.random.fold_in(seeds[8], 71), 0),
    }


RELAX = 0.8
DMIN_SQ = 0.25

def stencil(padded, zeta_field, diag_field):

    def pieces(field):
        center = field[..., 1:-1, 1:-1]
        second_x = field[..., 2:, 1:-1] + field[..., :-2, 1:-1] - 2.0 * center
        second_y = field[..., 1:-1, 2:] + field[..., 1:-1, :-2] - 2.0 * center
        mixed = 0.25 * (field[..., 2:, 2:] - field[..., 2:, :-2] - field[..., :-2, 2:] + field[..., :-2, :-2])
        return (center, second_x, second_y, mixed)
    part_u = pieces(padded[..., 0, :, :])
    part_v = pieces(padded[..., 1, :, :])
    along_u = diag_field * part_u[0] - 1.25 * zeta_field * part_u[1] - 0.25 * zeta_field * part_u[2] - zeta_field * part_v[3]
    along_v = diag_field * part_v[0] - 0.25 * zeta_field * part_v[1] - 1.25 * zeta_field * part_v[2] - zeta_field * part_u[3]
    return jnp.stack([along_u, along_v], axis=-3)

def precondition(vector, zeta_blocks, diag_blocks):
    diagonal_total = (diag_blocks + 3.0 * zeta_blocks)[:, None]
    iterate = vector / diagonal_total
    for relaxation in range(SWEEPS):
        padded = jnp.pad(iterate, ((0, 0), (0, 0), (1, 1), (1, 1)))
        iterate = iterate + RELAX * (vector - stencil(padded, zeta_blocks, diag_blocks)) / diagonal_total
    return iterate

def least_squares(hessenberg, start_norm):
    steps_count = hessenberg.shape[1]
    row_list = [hessenberg[i] for i in range(steps_count + 1)]
    target_vec = [start_norm] + [jnp.zeros((), jnp.float32) for i in range(steps_count)]
    for j in range(steps_count):
        upper = row_list[j][j]
        lower = row_list[j + 1][j]
        radius = jnp.sqrt(upper * upper + lower * lower)
        cosine = upper / radius
        sine_part = lower / radius
        first_row = cosine * row_list[j] + sine_part * row_list[j + 1]
        second_row = -sine_part * row_list[j] + cosine * row_list[j + 1]
        row_list[j], row_list[j + 1] = (first_row, second_row)
        first_val = cosine * target_vec[j] + sine_part * target_vec[j + 1]
        second_val = -sine_part * target_vec[j] + cosine * target_vec[j + 1]
        target_vec[j], target_vec[j + 1] = (first_val, second_val)
    weights_out = [None] * steps_count
    for j in range(steps_count - 1, -1, -1):
        accum = target_vec[j]
        for i in range(j + 1, steps_count):
            accum = accum - row_list[j][i] * weights_out[i]
        weights_out[j] = accum / row_list[j][j]
    return weights_out

def to_blocks(grid):
    channels = grid.shape[0]
    shaped = grid.reshape(channels, NX // BS, BS, NY // BS, BS).transpose(1, 3, 0, 2, 4)
    return shaped.reshape(NX // BS * (NY // BS), channels, BS, BS)

def from_blocks(blocks):
    channels = blocks.shape[1]
    shaped = blocks.reshape(NX // BS, NY // BS, channels, BS, BS).transpose(2, 0, 3, 1, 4)
    return shaped.reshape(channels, NX, NY)

def live_cells(ice_blocks):
    per_row = TY // BS
    tile_row = ice_blocks // BLOCKS_TILE
    inside = ice_blocks % BLOCKS_TILE
    block_row = (tile_row * (TX // BS) + inside // per_row).astype(jnp.int32)
    block_col = (jnp.arange(NCOL, dtype=jnp.int32)[:, None] * per_row + inside % per_row).astype(jnp.int32)
    grid_blocks = jnp.zeros((NX // BS, NY // BS), jnp.float32).at[block_row, block_col].set(1.0)
    return jnp.repeat(jnp.repeat(grid_blocks, BS, axis=0), BS, axis=1)

def reference(old_velocity, surface_stress, mass_term, ocean_drag, strength, ice_mask, ocean_mask, ice_blocks):
    padded = jnp.pad(old_velocity, ((0, 0), (1, 1), (1, 1)))
    flow_u = padded[0]
    flow_v = padded[1]
    strain_xx = 0.5 * (flow_u[2:, 1:-1] - flow_u[:-2, 1:-1])
    strain_yy = 0.5 * (flow_v[1:-1, 2:] - flow_v[1:-1, :-2])
    strain_xy = 0.25 * (flow_u[1:-1, 2:] - flow_u[1:-1, :-2] + flow_v[2:, 1:-1] - flow_v[:-2, 1:-1])
    deform_sq = 1.25 * (strain_xx * strain_xx + strain_yy * strain_yy) + strain_xy * strain_xy + 1.5 * strain_xx * strain_yy
    is_ocean = ocean_mask.astype(jnp.float32)
    zeta_field = is_ocean * ice_mask.astype(jnp.float32) * strength / (2.0 * jnp.sqrt(deform_sq + DMIN_SQ))
    diag_field = is_ocean * (mass_term + ocean_drag) + (1.0 - is_ocean)
    live = live_cells(ice_blocks)
    rhs = live * is_ocean * (surface_stress + mass_term * old_velocity)
    zeta_blocks = to_blocks(zeta_field[None])[:, 0]
    diag_blocks = to_blocks(diag_field[None])[:, 0]

    def system(vector):
        grown = jnp.pad(vector, ((0, 0), (1, 1), (1, 1)))
        return live * stencil(grown, zeta_field, diag_field)

    def apply_precond(vector):
        return from_blocks(precondition(to_blocks(vector), zeta_blocks, diag_blocks))
    solution = jnp.zeros_like(rhs)
    for restart in range(CYCLES):
        if restart == 0:
            residual = rhs
        else:
            residual = rhs - system(solution)
        start_norm = jnp.sqrt(jnp.sum(residual * residual))
        basis_list = [residual / start_norm]
        directions = []
        hessenberg = jnp.zeros((KRYLOV + 1, KRYLOV), jnp.float32)
        for arnoldi in range(KRYLOV):
            direction = apply_precond(basis_list[arnoldi])
            directions.append(direction)
            images = system(direction)
            products = jnp.stack([jnp.sum(images * vector) for vector in basis_list])
            for i in range(arnoldi + 1):
                images = images - products[i] * basis_list[i]
            new_norm = jnp.sqrt(jnp.sum(images * images))
            hessenberg = hessenberg.at[:arnoldi + 1, arnoldi].set(products).at[arnoldi + 1, arnoldi].set(new_norm)
            if arnoldi + 1 < KRYLOV:
                basis_list.append(images / new_norm)
        weights_out = least_squares(hessenberg, start_norm)
        for arnoldi in range(KRYLOV):
            solution = solution + weights_out[arnoldi] * directions[arnoldi]
    return solution
```

```python
import jax
import jax.numpy as jnp
from jax import lax
from jax.sharding import PartitionSpec as P

BS = 128
KRYLOV = 2
CYCLES = 2
SWEEPS = 2


RELAX = 0.8
DMIN_SQ = 0.25

COLS = ("chip", "grp")


def edges(array, axis, dim):
    size, length = (lax.axis_size(axis), array.shape[dim])
    up = [(i, i + 1) for i in range(size - 1)]
    down = [(j, i) for i, j in up]
    last = lax.slice_in_dim(array, length - 1, length, axis=dim)
    initial = lax.slice_in_dim(array, 0, 1, axis=dim)
    before = lax.ppermute(last, axis, up)
    after = lax.ppermute(initial, axis, down)
    return before, after


def extended(array):
    before, after = edges(array, "row", 1)
    array = jnp.concatenate([before, array, after], axis=1)
    before, after = edges(array, COLS, 2)
    return jnp.concatenate([before, array, after], axis=2)


def stencil(padded, zeta_field, diag_field):

    def pieces(field):
        center = field[..., 1:-1, 1:-1]
        second_x = field[..., 2:, 1:-1] + field[..., :-2, 1:-1] - 2.0 * center
        second_y = field[..., 1:-1, 2:] + field[..., 1:-1, :-2] - 2.0 * center
        mixed = 0.25 * (
            field[..., 2:, 2:] - field[..., 2:, :-2] - field[..., :-2, 2:] + field[..., :-2, :-2]
        )
        return (center, second_x, second_y, mixed)

    part_u = pieces(padded[..., 0, :, :])
    part_v = pieces(padded[..., 1, :, :])
    along_u = (
        diag_field * part_u[0]
        - 1.25 * zeta_field * part_u[1]
        - 0.25 * zeta_field * part_u[2]
        - zeta_field * part_v[3]
    )
    along_v = (
        diag_field * part_v[0]
        - 0.25 * zeta_field * part_v[1]
        - 1.25 * zeta_field * part_v[2]
        - zeta_field * part_u[3]
    )
    return jnp.stack([along_u, along_v], axis=-3)


def grid_to_blocks(tile_grid):
    channels, tile_rows, tile_cols = tile_grid.shape
    shaped = tile_grid.reshape(channels, tile_rows // BS, BS, tile_cols // BS, BS).transpose(
        1, 3, 0, 2, 4
    )
    return shaped.reshape(tile_rows // BS * (tile_cols // BS), channels, BS, BS)


def blocks_to_grid(blocks, tile_rows, tile_cols):
    channels = blocks.shape[1]
    shaped = blocks.reshape(tile_rows // BS, tile_cols // BS, channels, BS, BS).transpose(
        2, 0, 3, 1, 4
    )
    return shaped.reshape(channels, tile_rows, tile_cols)


def precondition(vector, zeta_blocks, diag_blocks):
    diagonal_total = (diag_blocks + 3.0 * zeta_blocks)[:, None]
    iterate = vector / diagonal_total
    for relaxation in range(SWEEPS):
        padded = jnp.pad(iterate, ((0, 0), (0, 0), (1, 1), (1, 1)))
        iterate = (
            iterate + RELAX * (vector - stencil(padded, zeta_blocks, diag_blocks)) / diagonal_total
        )
    return iterate


def least_squares(h, start_norm):
    steps_count = KRYLOV
    row_list = [[h[i][j] for j in range(steps_count)] for i in range(steps_count + 1)]
    target_vec = [start_norm] + [jnp.zeros((), jnp.float32) for i in range(steps_count)]
    for j in range(steps_count):
        upper = row_list[j][j]
        lower = row_list[j + 1][j]
        radius = jnp.sqrt(upper * upper + lower * lower)
        cosine = upper / radius
        sine_part = lower / radius
        first_row = [cosine * p + sine_part * q for p, q in zip(row_list[j], row_list[j + 1])]
        second_row = [-sine_part * p + cosine * q for p, q in zip(row_list[j], row_list[j + 1])]
        row_list[j], row_list[j + 1] = (first_row, second_row)
        first_val = cosine * target_vec[j] + sine_part * target_vec[j + 1]
        second_val = -sine_part * target_vec[j] + cosine * target_vec[j + 1]
        target_vec[j], target_vec[j + 1] = (first_val, second_val)
    weights_out = [None] * steps_count
    for j in range(steps_count - 1, -1, -1):
        accum = target_vec[j]
        for i in range(j + 1, steps_count):
            accum = accum - row_list[j][i] * weights_out[i]
        weights_out[j] = accum / row_list[j][j]
    return weights_out


def cycle_coefficients(gram):
    count = len(gram)

    def dot(p, q):
        total = None
        for i in range(count):
            for j in range(count):
                term = p[i] * gram[i][j] * q[j]
                total = term if total is None else total + term
        return total

    def shift(p):
        return [jnp.zeros((), jnp.float32)] + p[:-1]

    def scale(p, s):
        return [x * s for x in p]

    def axpy(p, s, q):
        return [x - s * y for x, y in zip(p, q)]

    one = jnp.ones((), jnp.float32)
    zero = jnp.zeros((), jnp.float32)
    start = [one] + [zero] * (count - 1)
    start_norm = jnp.sqrt(dot(start, start))
    basis_list = [scale(start, 1.0 / start_norm)]
    images_list = []
    h = [[zero] * KRYLOV for _ in range(KRYLOV + 1)]
    for arnoldi in range(KRYLOV):
        images = shift(basis_list[arnoldi])
        images_list.append(images)
        products = [dot(images, vector) for vector in basis_list]
        for i in range(arnoldi + 1):
            images = axpy(images, products[i], basis_list[i])
        new_norm = jnp.sqrt(dot(images, images))
        for i in range(arnoldi + 1):
            h[i][arnoldi] = products[i]
        h[arnoldi + 1][arnoldi] = new_norm
        if arnoldi + 1 < KRYLOV:
            basis_list.append(scale(images, 1.0 / new_norm))
    weights_out = least_squares(h, start_norm)
    update = [zero] * count
    residual = list(start)
    for arnoldi in range(KRYLOV):
        update = [u + weights_out[arnoldi] * b for u, b in zip(update, basis_list[arnoldi])]
        residual = axpy(residual, weights_out[arnoldi], images_list[arnoldi])
    return update, residual


def butterfly(values, axis):
    size = lax.axis_size(axis)
    stride = 1
    while stride < size:
        values = values + lax.ppermute(values, axis, [(i, i ^ stride) for i in range(size)])
        stride *= 2
    return values


def reduce_all(values):
    return butterfly(butterfly(butterfly(values, "chip"), "row"), "grp")


def shards(
    old_velocity, surface_stress, mass_term, ocean_drag, strength, ice_mask, ocean_mask, ice_blocks
):
    tile_rows = old_velocity.shape[1]
    tile_cols = old_velocity.shape[2]
    per_row = tile_cols // BS
    tile_blocks = tile_rows // BS * per_row

    rows_before, rows_after = edges(old_velocity, "row", 1)
    cols_before, cols_after = edges(old_velocity, COLS, 2)
    along_x = jnp.concatenate([rows_before, old_velocity, rows_after], axis=1)
    along_y = jnp.concatenate([cols_before, old_velocity, cols_after], axis=2)
    strain_xx = 0.5 * (along_x[0, 2:, :] - along_x[0, :-2, :])
    strain_yy = 0.5 * (along_y[1, :, 2:] - along_y[1, :, :-2])
    strain_xy = 0.25 * (
        along_y[0, :, 2:] - along_y[0, :, :-2] + along_x[1, 2:, :] - along_x[1, :-2, :]
    )
    deform_sq = (
        1.25 * (strain_xx * strain_xx + strain_yy * strain_yy)
        + strain_xy * strain_xy
        + 1.5 * strain_xx * strain_yy
    )
    is_ocean = ocean_mask.astype(jnp.float32)
    zeta_tile = (
        is_ocean * ice_mask.astype(jnp.float32) * strength / (2.0 * jnp.sqrt(deform_sq + DMIN_SQ))
    )
    diag_tile = is_ocean * (mass_term + ocean_drag) + (1.0 - is_ocean)

    my_row = lax.axis_index("row")
    listed = ice_blocks[0]
    wanted = my_row * tile_blocks + jnp.arange(tile_blocks, dtype=jnp.int32)
    flags = jnp.any(listed[:, None] == wanted[None, :], axis=0).astype(jnp.float32)
    live = jnp.repeat(
        jnp.repeat(flags.reshape(tile_rows // BS, per_row), BS, axis=0), BS, axis=1
    )
    rhs = live * is_ocean * (surface_stress + mass_term * old_velocity)

    zeta_blocks = grid_to_blocks(zeta_tile[None])[:, 0]
    diag_blocks = grid_to_blocks(diag_tile[None])[:, 0]

    def apply_system(vector):
        return live * stencil(extended(vector), zeta_tile, diag_tile)

    def apply_precond(vector):
        return blocks_to_grid(
            precondition(grid_to_blocks(vector), zeta_blocks, diag_blocks), tile_rows, tile_cols
        )

    solution = jnp.zeros_like(rhs)
    residual = rhs
    for restart in range(CYCLES):
        krylov = [residual]
        directions = []
        for step in range(KRYLOV):
            directions.append(apply_precond(krylov[-1]))
            krylov.append(apply_system(directions[-1]))
        count = len(krylov)
        pairs = [(i, j) for i in range(count) for j in range(i, count)]
        local = jnp.stack([jnp.sum(krylov[i] * krylov[j]) for i, j in pairs])
        total = reduce_all(local)
        gram = [[None] * count for _ in range(count)]
        for index, (i, j) in enumerate(pairs):
            gram[i][j] = total[index]
            gram[j][i] = total[index]
        update, left = cycle_coefficients(gram)
        for i in range(KRYLOV):
            solution = solution + update[i] * directions[i]
        if restart + 1 < CYCLES:
            combined = left[0] * krylov[0]
            for i in range(1, count):
                combined = combined + left[i] * krylov[i]
            residual = combined
    return solution


def solution(mesh):
    return jax.shard_map(
        shards,
        mesh=mesh,
        in_specs=(
            P(None, "row", COLS),
            P(None, "row", COLS),
            P("row", COLS),
            P("row", COLS),
            P("row", COLS),
            P("row", COLS),
            P("row", COLS),
            P(COLS, None),
        ),
        out_specs=P(None, "row", COLS),
        check_vma=False,
    )
```

```python
import jax
import jax.numpy as jnp
from jax import lax
from jax.experimental import pallas as pl
from jax.experimental.pallas import tpu as pltpu
from jax.sharding import PartitionSpec as P

BS = 128
KRYLOV = 2
CYCLES = 2
SWEEPS = 2


RELAX = 0.8
DMIN_SQ = 0.25

COLS = ("chip", "grp")


def edges(array, axis, dim):
    size, length = (lax.axis_size(axis), array.shape[dim])
    up = [(i, i + 1) for i in range(size - 1)]
    down = [(j, i) for i, j in up]
    last = lax.slice_in_dim(array, length - 1, length, axis=dim)
    initial = lax.slice_in_dim(array, 0, 1, axis=dim)
    before = lax.ppermute(last, axis, up)
    after = lax.ppermute(initial, axis, down)
    return before, after


def extended(array):
    before, after = edges(array, "row", 1)
    array = jnp.concatenate([before, array, after], axis=1)
    before, after = edges(array, COLS, 2)
    return jnp.concatenate([before, array, after], axis=2)


def stencil(padded, zeta_field, diag_field):

    def pieces(field):
        center = field[..., 1:-1, 1:-1]
        second_x = field[..., 2:, 1:-1] + field[..., :-2, 1:-1] - 2.0 * center
        second_y = field[..., 1:-1, 2:] + field[..., 1:-1, :-2] - 2.0 * center
        mixed = 0.25 * (
            field[..., 2:, 2:] - field[..., 2:, :-2] - field[..., :-2, 2:] + field[..., :-2, :-2]
        )
        return (center, second_x, second_y, mixed)

    part_u = pieces(padded[..., 0, :, :])
    part_v = pieces(padded[..., 1, :, :])
    along_u = (
        diag_field * part_u[0]
        - 1.25 * zeta_field * part_u[1]
        - 0.25 * zeta_field * part_u[2]
        - zeta_field * part_v[3]
    )
    along_v = (
        diag_field * part_v[0]
        - 0.25 * zeta_field * part_v[1]
        - 1.25 * zeta_field * part_v[2]
        - zeta_field * part_u[3]
    )
    return jnp.stack([along_u, along_v], axis=-3)


def grid_to_blocks(tile_grid):
    channels, tile_rows, tile_cols = tile_grid.shape
    shaped = tile_grid.reshape(channels, tile_rows // BS, BS, tile_cols // BS, BS).transpose(
        1, 3, 0, 2, 4
    )
    return shaped.reshape(tile_rows // BS * (tile_cols // BS), channels, BS, BS)


def blocks_to_grid(blocks, tile_rows, tile_cols):
    channels = blocks.shape[1]
    shaped = blocks.reshape(tile_rows // BS, tile_cols // BS, channels, BS, BS).transpose(
        2, 0, 3, 1, 4
    )
    return shaped.reshape(channels, tile_rows, tile_cols)


def precondition(vector, zeta_blocks, diag_blocks):
    diagonal_total = (diag_blocks + 3.0 * zeta_blocks)[:, None]
    iterate = vector / diagonal_total
    for relaxation in range(SWEEPS):
        padded = jnp.pad(iterate, ((0, 0), (0, 0), (1, 1), (1, 1)))
        iterate = (
            iterate + RELAX * (vector - stencil(padded, zeta_blocks, diag_blocks)) / diagonal_total
        )
    return iterate


def least_squares(h, start_norm):
    steps_count = KRYLOV
    row_list = [[h[i][j] for j in range(steps_count)] for i in range(steps_count + 1)]
    target_vec = [start_norm] + [jnp.zeros_like(start_norm) for i in range(steps_count)]
    for j in range(steps_count):
        upper = row_list[j][j]
        lower = row_list[j + 1][j]
        radius = jnp.sqrt(upper * upper + lower * lower)
        cosine = upper / radius
        sine_part = lower / radius
        first_row = [cosine * p + sine_part * q for p, q in zip(row_list[j], row_list[j + 1])]
        second_row = [-sine_part * p + cosine * q for p, q in zip(row_list[j], row_list[j + 1])]
        row_list[j], row_list[j + 1] = (first_row, second_row)
        first_val = cosine * target_vec[j] + sine_part * target_vec[j + 1]
        second_val = -sine_part * target_vec[j] + cosine * target_vec[j + 1]
        target_vec[j], target_vec[j + 1] = (first_val, second_val)
    weights_out = [None] * steps_count
    for j in range(steps_count - 1, -1, -1):
        accum = target_vec[j]
        for i in range(j + 1, steps_count):
            accum = accum - row_list[j][i] * weights_out[i]
        weights_out[j] = accum / row_list[j][j]
    return weights_out


def cycle_coefficients(gram):
    count = len(gram)

    def dot(p, q):
        total = None
        for i in range(count):
            for j in range(count):
                term = p[i] * gram[i][j] * q[j]
                total = term if total is None else total + term
        return total

    def shift(p):
        return [jnp.zeros_like(p[0])] + p[:-1]

    def scale(p, s):
        return [x * s for x in p]

    def axpy(p, s, q):
        return [x - s * y for x, y in zip(p, q)]

    one = jnp.ones_like(gram[0][0])
    zero = jnp.zeros_like(gram[0][0])
    start = [one] + [zero] * (count - 1)
    start_norm = jnp.sqrt(dot(start, start))
    basis_list = [scale(start, 1.0 / start_norm)]
    images_list = []
    h = [[zero] * KRYLOV for _ in range(KRYLOV + 1)]
    for arnoldi in range(KRYLOV):
        images = shift(basis_list[arnoldi])
        images_list.append(images)
        products = [dot(images, vector) for vector in basis_list]
        for i in range(arnoldi + 1):
            images = axpy(images, products[i], basis_list[i])
        new_norm = jnp.sqrt(dot(images, images))
        for i in range(arnoldi + 1):
            h[i][arnoldi] = products[i]
        h[arnoldi + 1][arnoldi] = new_norm
        if arnoldi + 1 < KRYLOV:
            basis_list.append(scale(images, 1.0 / new_norm))
    weights_out = least_squares(h, start_norm)
    update = [zero] * count
    residual = list(start)
    for arnoldi in range(KRYLOV):
        update = [u + weights_out[arnoldi] * b for u, b in zip(update, basis_list[arnoldi])]
        residual = axpy(residual, weights_out[arnoldi], images_list[arnoldi])
    return update, residual


def coefficients_kernel(count, total_ref, out_ref):
    shape = out_ref.shape
    pairs = [(i, j) for i in range(count) for j in range(i, count)]
    gram = [[None] * count for _ in range(count)]
    for index, (i, j) in enumerate(pairs):
        value = jnp.full(shape, total_ref[index], jnp.float32)
        gram[i][j] = value
        gram[j][i] = value
    update, left = cycle_coefficients(gram)
    rows = lax.broadcasted_iota(jnp.int32, shape, 0)
    result = jnp.zeros(shape, jnp.float32)
    for k, value in enumerate(update[:KRYLOV] + left):
        result = jnp.where(rows == k, value, result)
    out_ref[...] = result


def solve_small(total, count):
    out = pl.pallas_call(
        lambda total_ref, out_ref: coefficients_kernel(count, total_ref, out_ref),
        out_shape=jax.ShapeDtypeStruct((8, 128), jnp.float32),
        in_specs=[pl.BlockSpec(memory_space=pltpu.SMEM)],
        out_specs=pl.BlockSpec(memory_space=pltpu.VMEM),
    )(total)
    column = out[:, 0]
    return [column[k] for k in range(KRYLOV)], [column[KRYLOV + k] for k in range(count)]


def butterfly(values, axis):
    size = lax.axis_size(axis)
    stride = 1
    while stride < size:
        values = values + lax.ppermute(values, axis, [(i, i ^ stride) for i in range(size)])
        stride *= 2
    return values


def reduce_all(values):
    return butterfly(butterfly(butterfly(values, "chip"), "row"), "grp")


def shards(
    old_velocity, surface_stress, mass_term, ocean_drag, strength, ice_mask, ocean_mask, ice_blocks
):
    tile_rows = old_velocity.shape[1]
    tile_cols = old_velocity.shape[2]
    per_row = tile_cols // BS
    tile_blocks = tile_rows // BS * per_row

    rows_before, rows_after = edges(old_velocity, "row", 1)
    cols_before, cols_after = edges(old_velocity, COLS, 2)
    along_x = jnp.concatenate([rows_before, old_velocity, rows_after], axis=1)
    along_y = jnp.concatenate([cols_before, old_velocity, cols_after], axis=2)
    strain_xx = 0.5 * (along_x[0, 2:, :] - along_x[0, :-2, :])
    strain_yy = 0.5 * (along_y[1, :, 2:] - along_y[1, :, :-2])
    strain_xy = 0.25 * (
        along_y[0, :, 2:] - along_y[0, :, :-2] + along_x[1, 2:, :] - along_x[1, :-2, :]
    )
    deform_sq = (
        1.25 * (strain_xx * strain_xx + strain_yy * strain_yy)
        + strain_xy * strain_xy
        + 1.5 * strain_xx * strain_yy
    )
    is_ocean = ocean_mask.astype(jnp.float32)
    zeta_tile = (
        is_ocean * ice_mask.astype(jnp.float32) * strength / (2.0 * jnp.sqrt(deform_sq + DMIN_SQ))
    )
    diag_tile = is_ocean * (mass_term + ocean_drag) + (1.0 - is_ocean)

    my_row = lax.axis_index("row")
    listed = ice_blocks[0]
    wanted = my_row * tile_blocks + jnp.arange(tile_blocks, dtype=jnp.int32)
    flags = jnp.any(listed[:, None] == wanted[None, :], axis=0).astype(jnp.float32)
    live = jnp.repeat(
        jnp.repeat(flags.reshape(tile_rows // BS, per_row), BS, axis=0), BS, axis=1
    )
    rhs = live * is_ocean * (surface_stress + mass_term * old_velocity)

    zeta_blocks = grid_to_blocks(zeta_tile[None])[:, 0]
    diag_blocks = grid_to_blocks(diag_tile[None])[:, 0]

    def apply_system(vector):
        return live * stencil(extended(vector), zeta_tile, diag_tile)

    def apply_precond(vector):
        return blocks_to_grid(
            precondition(grid_to_blocks(vector), zeta_blocks, diag_blocks), tile_rows, tile_cols
        )

    solution = jnp.zeros_like(rhs)
    residual = rhs
    for restart in range(CYCLES):
        krylov = [residual]
        directions = []
        for step in range(KRYLOV):
            directions.append(apply_precond(krylov[-1]))
            krylov.append(apply_system(directions[-1]))
        count = len(krylov)
        pairs = [(i, j) for i in range(count) for j in range(i, count)]
        local = jnp.stack([jnp.sum(krylov[i] * krylov[j]) for i, j in pairs])
        total = reduce_all(local)
        update, left = solve_small(total, count)
        for i in range(KRYLOV):
            solution = solution + update[i] * directions[i]
        if restart + 1 < CYCLES:
            combined = left[0] * krylov[0]
            for i in range(1, count):
                combined = combined + left[i] * krylov[i]
            residual = combined
    return solution


def solution(mesh):
    return jax.shard_map(
        shards,
        mesh=mesh,
        in_specs=(
            P(None, "row", COLS),
            P(None, "row", COLS),
            P("row", COLS),
            P("row", COLS),
            P("row", COLS),
            P("row", COLS),
            P("row", COLS),
            P(COLS, None),
        ),
        out_specs=P(None, "row", COLS),
        check_vma=False,
    )
```

```python
import jax
import jax.numpy as jnp
from jax import lax
from jax.experimental import pallas as pl
from jax.experimental.pallas import tpu as pltpu
from jax.sharding import PartitionSpec as P

BS = 128
KRYLOV = 2
CYCLES = 2
SWEEPS = 2


RELAX = 0.8
DMIN_SQ = 0.25
SHIFT = 1.0

COLS = ("chip", "grp")


def edges(array, axis, dim):
    size, length = (lax.axis_size(axis), array.shape[dim])
    up = [(i, i + 1) for i in range(size - 1)]
    down = [(j, i) for i, j in up]
    last = lax.slice_in_dim(array, length - 1, length, axis=dim)
    initial = lax.slice_in_dim(array, 0, 1, axis=dim)
    before = lax.ppermute(last, axis, up)
    after = lax.ppermute(initial, axis, down)
    return before, after


def extended(array):
    before, after = edges(array, "row", 1)
    array = jnp.concatenate([before, array, after], axis=1)
    before, after = edges(array, COLS, 2)
    return jnp.concatenate([before, array, after], axis=2)


def stencil(padded, zeta_field, diag_field):

    def pieces(field):
        center = field[..., 1:-1, 1:-1]
        second_x = field[..., 2:, 1:-1] + field[..., :-2, 1:-1] - 2.0 * center
        second_y = field[..., 1:-1, 2:] + field[..., 1:-1, :-2] - 2.0 * center
        mixed = 0.25 * (
            field[..., 2:, 2:] - field[..., 2:, :-2] - field[..., :-2, 2:] + field[..., :-2, :-2]
        )
        return (center, second_x, second_y, mixed)

    part_u = pieces(padded[..., 0, :, :])
    part_v = pieces(padded[..., 1, :, :])
    along_u = (
        diag_field * part_u[0]
        - 1.25 * zeta_field * part_u[1]
        - 0.25 * zeta_field * part_u[2]
        - zeta_field * part_v[3]
    )
    along_v = (
        diag_field * part_v[0]
        - 0.25 * zeta_field * part_v[1]
        - 1.25 * zeta_field * part_v[2]
        - zeta_field * part_u[3]
    )
    return jnp.stack([along_u, along_v], axis=-3)


def grid_to_blocks(tile_grid):
    channels, tile_rows, tile_cols = tile_grid.shape
    shaped = tile_grid.reshape(channels, tile_rows // BS, BS, tile_cols // BS, BS).transpose(
        1, 3, 0, 2, 4
    )
    return shaped.reshape(tile_rows // BS * (tile_cols // BS), channels, BS, BS)


def blocks_to_grid(blocks, tile_rows, tile_cols):
    channels = blocks.shape[1]
    shaped = blocks.reshape(tile_rows // BS, tile_cols // BS, channels, BS, BS).transpose(
        2, 0, 3, 1, 4
    )
    return shaped.reshape(channels, tile_rows, tile_cols)


def precondition(vector, zeta_blocks, diag_blocks):
    diagonal_total = (diag_blocks + 3.0 * zeta_blocks)[:, None]
    iterate = vector / diagonal_total
    for relaxation in range(SWEEPS):
        padded = jnp.pad(iterate, ((0, 0), (0, 0), (1, 1), (1, 1)))
        iterate = (
            iterate + RELAX * (vector - stencil(padded, zeta_blocks, diag_blocks)) / diagonal_total
        )
    return iterate


def least_squares(h, start_norm):
    steps_count = KRYLOV
    row_list = [[h[i][j] for j in range(steps_count)] for i in range(steps_count + 1)]
    target_vec = [start_norm] + [jnp.zeros_like(start_norm) for i in range(steps_count)]
    for j in range(steps_count):
        upper = row_list[j][j]
        lower = row_list[j + 1][j]
        radius = jnp.sqrt(upper * upper + lower * lower)
        cosine = upper / radius
        sine_part = lower / radius
        first_row = [cosine * p + sine_part * q for p, q in zip(row_list[j], row_list[j + 1])]
        second_row = [-sine_part * p + cosine * q for p, q in zip(row_list[j], row_list[j + 1])]
        row_list[j], row_list[j + 1] = (first_row, second_row)
        first_val = cosine * target_vec[j] + sine_part * target_vec[j + 1]
        second_val = -sine_part * target_vec[j] + cosine * target_vec[j + 1]
        target_vec[j], target_vec[j + 1] = (first_val, second_val)
    weights_out = [None] * steps_count
    for j in range(steps_count - 1, -1, -1):
        accum = target_vec[j]
        for i in range(j + 1, steps_count):
            accum = accum - row_list[j][i] * weights_out[i]
        weights_out[j] = accum / row_list[j][j]
    return weights_out


def krylov_coefficients(gram):
    count = len(gram)

    def dot(p, q):
        total = None
        for i in range(count):
            for j in range(count):
                term = p[i] * gram[i][j] * q[j]
                total = term if total is None else total + term
        return total

    def shift(p):
        return [SHIFT * p[0]] + [x + SHIFT * y for x, y in zip(p[:-1], p[1:])]

    def scale(p, s):
        return [x * s for x in p]

    def axpy(p, s, q):
        return [x - s * y for x, y in zip(p, q)]

    one = jnp.ones_like(gram[0][0])
    zero = jnp.zeros_like(gram[0][0])
    residual = [one] + [zero] * (count - 1)
    solution = [zero] * count
    for restart in range(CYCLES):
        start_norm = jnp.sqrt(dot(residual, residual))
        basis_list = [scale(residual, 1.0 / start_norm)]
        images_list = []
        h = [[zero] * KRYLOV for _ in range(KRYLOV + 1)]
        for arnoldi in range(KRYLOV):
            images = shift(basis_list[arnoldi])
            images_list.append(images)
            products = [dot(images, vector) for vector in basis_list]
            for i in range(arnoldi + 1):
                images = axpy(images, products[i], basis_list[i])
            new_norm = jnp.sqrt(dot(images, images))
            for i in range(arnoldi + 1):
                h[i][arnoldi] = products[i]
            h[arnoldi + 1][arnoldi] = new_norm
            if arnoldi + 1 < KRYLOV:
                basis_list.append(scale(images, 1.0 / new_norm))
        weights_out = least_squares(h, start_norm)
        for arnoldi in range(KRYLOV):
            solution = [u + weights_out[arnoldi] * b for u, b in zip(solution, basis_list[arnoldi])]
            residual = axpy(residual, weights_out[arnoldi], images_list[arnoldi])
    return solution


def gram_kernel(count, *refs):
    vectors = [refs[i][...] for i in range(count)]
    out_ref = refs[count]
    shape = out_ref.shape
    rows = lax.broadcasted_iota(jnp.int32, shape, 0)
    lanes = lax.broadcasted_iota(jnp.int32, shape, 1)
    result = jnp.zeros(shape, jnp.float32)
    index = 0
    for i in range(count):
        for j in range(i, count):
            product = vectors[i] * vectors[j]
            part = jnp.sum(jnp.sum(product, axis=0, keepdims=True), axis=1, keepdims=True)
            result = jnp.where((rows == 0) & (lanes == index), part, result)
            index += 1
    out_ref[...] = result


def local_gram(krylov):
    count = len(krylov)
    flat = [k.reshape(-1, k.shape[-1]) for k in krylov]
    return pl.pallas_call(
        lambda *refs: gram_kernel(count, *refs),
        out_shape=jax.ShapeDtypeStruct((8, 128), jnp.float32),
        in_specs=[pl.BlockSpec(memory_space=pltpu.VMEM)] * count,
        out_specs=pl.BlockSpec(memory_space=pltpu.VMEM),
    )(*flat)


def coefficients_kernel(count, total_ref, out_ref):
    shape = out_ref.shape
    pairs = [(i, j) for i in range(count) for j in range(i, count)]
    gram = [[None] * count for _ in range(count)]
    for index, (i, j) in enumerate(pairs):
        value = jnp.full(shape, total_ref[0, index], jnp.float32)
        gram[i][j] = value
        gram[j][i] = value
    update = krylov_coefficients(gram)
    rows = lax.broadcasted_iota(jnp.int32, shape, 0)
    result = jnp.zeros(shape, jnp.float32)
    for k, value in enumerate(update[: count - 1]):
        result = jnp.where(rows == k, value, result)
    out_ref[...] = result


def solve_small(total, count):
    out = pl.pallas_call(
        lambda total_ref, out_ref: coefficients_kernel(count, total_ref, out_ref),
        out_shape=jax.ShapeDtypeStruct((8, 128), jnp.float32),
        in_specs=[pl.BlockSpec(memory_space=pltpu.SMEM)],
        out_specs=pl.BlockSpec(memory_space=pltpu.VMEM),
    )(total)
    column = out[:, 0]
    return [column[k] for k in range(count - 1)]


def butterfly(values, axis):
    size = lax.axis_size(axis)
    stride = 1
    while stride < size:
        values = values + lax.ppermute(values, axis, [(i, i ^ stride) for i in range(size)])
        stride *= 2
    return values


def reduce_all(values):
    return butterfly(butterfly(butterfly(values, "chip"), "row"), "grp")


def shards(
    old_velocity, surface_stress, mass_term, ocean_drag, strength, ice_mask, ocean_mask, ice_blocks
):
    tile_rows = old_velocity.shape[1]
    tile_cols = old_velocity.shape[2]
    per_row = tile_cols // BS
    tile_blocks = tile_rows // BS * per_row

    rows_before, rows_after = edges(old_velocity, "row", 1)
    cols_before, cols_after = edges(old_velocity, COLS, 2)
    along_x = jnp.concatenate([rows_before, old_velocity, rows_after], axis=1)
    along_y = jnp.concatenate([cols_before, old_velocity, cols_after], axis=2)
    strain_xx = 0.5 * (along_x[0, 2:, :] - along_x[0, :-2, :])
    strain_yy = 0.5 * (along_y[1, :, 2:] - along_y[1, :, :-2])
    strain_xy = 0.25 * (
        along_y[0, :, 2:] - along_y[0, :, :-2] + along_x[1, 2:, :] - along_x[1, :-2, :]
    )
    deform_sq = (
        1.25 * (strain_xx * strain_xx + strain_yy * strain_yy)
        + strain_xy * strain_xy
        + 1.5 * strain_xx * strain_yy
    )
    is_ocean = ocean_mask.astype(jnp.float32)
    zeta_tile = (
        is_ocean * ice_mask.astype(jnp.float32) * strength / (2.0 * jnp.sqrt(deform_sq + DMIN_SQ))
    )
    diag_tile = is_ocean * (mass_term + ocean_drag) + (1.0 - is_ocean)

    my_row = lax.axis_index("row")
    listed = ice_blocks[0]
    wanted = my_row * tile_blocks + jnp.arange(tile_blocks, dtype=jnp.int32)
    flags = jnp.any(listed[:, None] == wanted[None, :], axis=0).astype(jnp.float32)
    live = jnp.repeat(
        jnp.repeat(flags.reshape(tile_rows // BS, per_row), BS, axis=0), BS, axis=1
    )
    rhs = live * is_ocean * (surface_stress + mass_term * old_velocity)

    zeta_blocks = grid_to_blocks(zeta_tile[None])[:, 0]
    diag_blocks = grid_to_blocks(diag_tile[None])[:, 0]

    def apply_system(vector):
        return live * stencil(extended(vector), zeta_tile, diag_tile)

    def apply_precond(vector):
        return blocks_to_grid(
            precondition(grid_to_blocks(vector), zeta_blocks, diag_blocks), tile_rows, tile_cols
        )

    krylov = [rhs]
    directions = []
    for step in range(CYCLES * KRYLOV):
        directions.append(apply_precond(krylov[-1]))
        krylov.append(apply_system(directions[-1]) - SHIFT * krylov[-1])
    total = reduce_all(local_gram(krylov))
    update = solve_small(total, len(krylov))
    solution = update[0] * directions[0]
    for i in range(1, len(directions)):
        solution = solution + update[i] * directions[i]
    return solution


def solution(mesh):
    return jax.shard_map(
        shards,
        mesh=mesh,
        in_specs=(
            P(None, "row", COLS),
            P(None, "row", COLS),
            P("row", COLS),
            P("row", COLS),
            P("row", COLS),
            P("row", COLS),
            P("row", COLS),
            P(COLS, None),
        ),
        out_specs=P(None, "row", COLS),
        check_vma=False,
    )
```

```python
import jax
import jax.numpy as jnp
from jax import lax
from jax.experimental import pallas as pl
from jax.experimental.pallas import tpu as pltpu
from jax.sharding import PartitionSpec as P

BS = 128
KRYLOV = 2
CYCLES = 2
SWEEPS = 2


RELAX = 0.8
DMIN_SQ = 0.25
SHIFT = 1.0

COLS = ("chip", "grp")


def edges(array, axis, dim):
    size, length = (lax.axis_size(axis), array.shape[dim])
    up = [(i, i + 1) for i in range(size - 1)]
    down = [(j, i) for i, j in up]
    last = lax.slice_in_dim(array, length - 1, length, axis=dim)
    initial = lax.slice_in_dim(array, 0, 1, axis=dim)
    before = lax.ppermute(last, axis, up)
    after = lax.ppermute(initial, axis, down)
    return before, after


def extended(array):
    before, after = edges(array, "row", 1)
    array = jnp.concatenate([before, array, after], axis=1)
    before, after = edges(array, COLS, 2)
    return jnp.concatenate([before, array, after], axis=2)


def stencil(padded, zeta_field, diag_field):

    def pieces(field):
        center = field[..., 1:-1, 1:-1]
        second_x = field[..., 2:, 1:-1] + field[..., :-2, 1:-1] - 2.0 * center
        second_y = field[..., 1:-1, 2:] + field[..., 1:-1, :-2] - 2.0 * center
        mixed = 0.25 * (
            field[..., 2:, 2:] - field[..., 2:, :-2] - field[..., :-2, 2:] + field[..., :-2, :-2]
        )
        return (center, second_x, second_y, mixed)

    part_u = pieces(padded[..., 0, :, :])
    part_v = pieces(padded[..., 1, :, :])
    along_u = (
        diag_field * part_u[0]
        - 1.25 * zeta_field * part_u[1]
        - 0.25 * zeta_field * part_u[2]
        - zeta_field * part_v[3]
    )
    along_v = (
        diag_field * part_v[0]
        - 0.25 * zeta_field * part_v[1]
        - 1.25 * zeta_field * part_v[2]
        - zeta_field * part_u[3]
    )
    return jnp.stack([along_u, along_v], axis=-3)


def block_stencil(field, zeta_field, diag_field):
    rows = lax.broadcasted_iota(jnp.int32, field.shape[-2:], 0) % BS
    cols = lax.broadcasted_iota(jnp.int32, field.shape[-2:], 1) % BS
    padded = jnp.pad(field, ((0, 0), (1, 1), (1, 1)))
    height, width = field.shape[-2:]

    def neighbour(di, dj):
        inside = jnp.ones(field.shape[-2:], jnp.bool_)
        if di:
            inside = inside & (rows != (BS - 1 if di > 0 else 0))
        if dj:
            inside = inside & (cols != (BS - 1 if dj > 0 else 0))
        window = padded[:, 1 + di : 1 + di + height, 1 + dj : 1 + dj + width]
        return jnp.where(inside, window, 0.0)

    def pieces(channel):
        center = field[channel]
        second_x = neighbour(1, 0)[channel] + neighbour(-1, 0)[channel] - 2.0 * center
        second_y = neighbour(0, 1)[channel] + neighbour(0, -1)[channel] - 2.0 * center
        mixed = 0.25 * (
            neighbour(1, 1)[channel]
            - neighbour(1, -1)[channel]
            - neighbour(-1, 1)[channel]
            + neighbour(-1, -1)[channel]
        )
        return (center, second_x, second_y, mixed)

    part_u = pieces(0)
    part_v = pieces(1)
    along_u = (
        diag_field * part_u[0]
        - 1.25 * zeta_field * part_u[1]
        - 0.25 * zeta_field * part_u[2]
        - zeta_field * part_v[3]
    )
    along_v = (
        diag_field * part_v[0]
        - 0.25 * zeta_field * part_v[1]
        - 1.25 * zeta_field * part_v[2]
        - zeta_field * part_u[3]
    )
    return jnp.stack([along_u, along_v], axis=0)


def precondition(vector, zeta_field, diag_field):
    diagonal_total = diag_field + 3.0 * zeta_field
    iterate = vector / diagonal_total
    for relaxation in range(SWEEPS):
        iterate = (
            iterate
            + RELAX * (vector - block_stencil(iterate, zeta_field, diag_field)) / diagonal_total
        )
    return iterate


def least_squares(h, start_norm):
    steps_count = KRYLOV
    row_list = [[h[i][j] for j in range(steps_count)] for i in range(steps_count + 1)]
    target_vec = [start_norm] + [jnp.zeros_like(start_norm) for i in range(steps_count)]
    for j in range(steps_count):
        upper = row_list[j][j]
        lower = row_list[j + 1][j]
        radius = jnp.sqrt(upper * upper + lower * lower)
        cosine = upper / radius
        sine_part = lower / radius
        first_row = [cosine * p + sine_part * q for p, q in zip(row_list[j], row_list[j + 1])]
        second_row = [-sine_part * p + cosine * q for p, q in zip(row_list[j], row_list[j + 1])]
        row_list[j], row_list[j + 1] = (first_row, second_row)
        first_val = cosine * target_vec[j] + sine_part * target_vec[j + 1]
        second_val = -sine_part * target_vec[j] + cosine * target_vec[j + 1]
        target_vec[j], target_vec[j + 1] = (first_val, second_val)
    weights_out = [None] * steps_count
    for j in range(steps_count - 1, -1, -1):
        accum = target_vec[j]
        for i in range(j + 1, steps_count):
            accum = accum - row_list[j][i] * weights_out[i]
        weights_out[j] = accum / row_list[j][j]
    return weights_out


def krylov_coefficients(gram):
    count = len(gram)

    def dot(p, q):
        total = None
        for i in range(count):
            for j in range(count):
                term = p[i] * gram[i][j] * q[j]
                total = term if total is None else total + term
        return total

    def shift(p):
        return [SHIFT * p[0]] + [x + SHIFT * y for x, y in zip(p[:-1], p[1:])]

    def scale(p, s):
        return [x * s for x in p]

    def axpy(p, s, q):
        return [x - s * y for x, y in zip(p, q)]

    one = jnp.ones_like(gram[0][0])
    zero = jnp.zeros_like(gram[0][0])
    residual = [one] + [zero] * (count - 1)
    solution = [zero] * count
    for restart in range(CYCLES):
        start_norm = jnp.sqrt(dot(residual, residual))
        basis_list = [scale(residual, 1.0 / start_norm)]
        images_list = []
        h = [[zero] * KRYLOV for _ in range(KRYLOV + 1)]
        for arnoldi in range(KRYLOV):
            images = shift(basis_list[arnoldi])
            images_list.append(images)
            products = [dot(images, vector) for vector in basis_list]
            for i in range(arnoldi + 1):
                images = axpy(images, products[i], basis_list[i])
            new_norm = jnp.sqrt(dot(images, images))
            for i in range(arnoldi + 1):
                h[i][arnoldi] = products[i]
            h[arnoldi + 1][arnoldi] = new_norm
            if arnoldi + 1 < KRYLOV:
                basis_list.append(scale(images, 1.0 / new_norm))
        weights_out = least_squares(h, start_norm)
        for arnoldi in range(KRYLOV):
            solution = [u + weights_out[arnoldi] * b for u, b in zip(solution, basis_list[arnoldi])]
            residual = axpy(residual, weights_out[arnoldi], images_list[arnoldi])
    return solution


def gram_kernel(count, *refs):
    vectors = [refs[i][...] for i in range(count)]
    out_ref = refs[count]
    shape = out_ref.shape
    rows = lax.broadcasted_iota(jnp.int32, shape, 0)
    lanes = lax.broadcasted_iota(jnp.int32, shape, 1)
    result = jnp.zeros(shape, jnp.float32)
    index = 0
    for i in range(count):
        for j in range(i, count):
            product = vectors[i] * vectors[j]
            part = jnp.sum(jnp.sum(product, axis=0, keepdims=True), axis=1, keepdims=True)
            result = jnp.where((rows == 0) & (lanes == index), part, result)
            index += 1
    out_ref[...] = result


def local_gram(krylov):
    count = len(krylov)
    flat = [k.reshape(-1, k.shape[-1]) for k in krylov]
    return pl.pallas_call(
        lambda *refs: gram_kernel(count, *refs),
        out_shape=jax.ShapeDtypeStruct((8, 128), jnp.float32),
        in_specs=[pl.BlockSpec(memory_space=pltpu.VMEM)] * count,
        out_specs=pl.BlockSpec(memory_space=pltpu.VMEM),
    )(*flat)


def coefficients_kernel(count, total_ref, out_ref):
    shape = out_ref.shape
    pairs = [(i, j) for i in range(count) for j in range(i, count)]
    gram = [[None] * count for _ in range(count)]
    for index, (i, j) in enumerate(pairs):
        value = jnp.full(shape, total_ref[0, index], jnp.float32)
        gram[i][j] = value
        gram[j][i] = value
    update = krylov_coefficients(gram)
    rows = lax.broadcasted_iota(jnp.int32, shape, 0)
    result = jnp.zeros(shape, jnp.float32)
    for k, value in enumerate(update[: count - 1]):
        result = jnp.where(rows == k, value, result)
    out_ref[...] = result


def solve_small(total, count):
    out = pl.pallas_call(
        lambda total_ref, out_ref: coefficients_kernel(count, total_ref, out_ref),
        out_shape=jax.ShapeDtypeStruct((8, 128), jnp.float32),
        in_specs=[pl.BlockSpec(memory_space=pltpu.SMEM)],
        out_specs=pl.BlockSpec(memory_space=pltpu.VMEM),
    )(total)
    column = out[:, 0]
    return [column[k] for k in range(count - 1)]


def butterfly(values, axis):
    size = lax.axis_size(axis)
    stride = 1
    while stride < size:
        values = values + lax.ppermute(values, axis, [(i, i ^ stride) for i in range(size)])
        stride *= 2
    return values


def reduce_all(values):
    return butterfly(butterfly(butterfly(values, "chip"), "row"), "grp")


def shards(
    old_velocity, surface_stress, mass_term, ocean_drag, strength, ice_mask, ocean_mask, ice_blocks
):
    tile_rows = old_velocity.shape[1]
    tile_cols = old_velocity.shape[2]
    per_row = tile_cols // BS
    tile_blocks = tile_rows // BS * per_row

    rows_before, rows_after = edges(old_velocity, "row", 1)
    cols_before, cols_after = edges(old_velocity, COLS, 2)
    along_x = jnp.concatenate([rows_before, old_velocity, rows_after], axis=1)
    along_y = jnp.concatenate([cols_before, old_velocity, cols_after], axis=2)
    strain_xx = 0.5 * (along_x[0, 2:, :] - along_x[0, :-2, :])
    strain_yy = 0.5 * (along_y[1, :, 2:] - along_y[1, :, :-2])
    strain_xy = 0.25 * (
        along_y[0, :, 2:] - along_y[0, :, :-2] + along_x[1, 2:, :] - along_x[1, :-2, :]
    )
    deform_sq = (
        1.25 * (strain_xx * strain_xx + strain_yy * strain_yy)
        + strain_xy * strain_xy
        + 1.5 * strain_xx * strain_yy
    )
    is_ocean = ocean_mask.astype(jnp.float32)
    zeta_tile = (
        is_ocean * ice_mask.astype(jnp.float32) * strength / (2.0 * jnp.sqrt(deform_sq + DMIN_SQ))
    )
    diag_tile = is_ocean * (mass_term + ocean_drag) + (1.0 - is_ocean)

    my_row = lax.axis_index("row")
    listed = ice_blocks[0]
    wanted = my_row * tile_blocks + jnp.arange(tile_blocks, dtype=jnp.int32)
    flags = jnp.any(listed[:, None] == wanted[None, :], axis=0).astype(jnp.float32)
    live = jnp.repeat(
        jnp.repeat(flags.reshape(tile_rows // BS, per_row), BS, axis=0), BS, axis=1
    )
    rhs = live * is_ocean * (surface_stress + mass_term * old_velocity)


    def apply_system(vector):
        return live * stencil(extended(vector), zeta_tile, diag_tile)

    def apply_precond(vector):
        return precondition(vector, zeta_tile, diag_tile)

    krylov = [rhs]
    directions = []
    for step in range(CYCLES * KRYLOV):
        directions.append(apply_precond(krylov[-1]))
        krylov.append(apply_system(directions[-1]) - SHIFT * krylov[-1])
    total = reduce_all(local_gram(krylov))
    update = solve_small(total, len(krylov))
    solution = update[0] * directions[0]
    for i in range(1, len(directions)):
        solution = solution + update[i] * directions[i]
    return solution


def solution(mesh):
    return jax.shard_map(
        shards,
        mesh=mesh,
        in_specs=(
            P(None, "row", COLS),
            P(None, "row", COLS),
            P("row", COLS),
            P("row", COLS),
            P("row", COLS),
            P("row", COLS),
            P("row", COLS),
            P(COLS, None),
        ),
        out_specs=P(None, "row", COLS),
        check_vma=False,
    )
```

```python
import jax
import jax.numpy as jnp
from jax import lax
from jax.experimental import pallas as pl
from jax.experimental.pallas import tpu as pltpu
from jax.sharding import PartitionSpec as P

BS = 128
KRYLOV = 2
CYCLES = 2
SWEEPS = 2


RELAX = 0.8
DMIN_SQ = 0.25
SHIFT = 1.0

COLS = ("chip", "grp")


def stencil(padded, zeta_field, diag_field):

    def pieces(field):
        center = field[..., 1:-1, 1:-1]
        second_x = field[..., 2:, 1:-1] + field[..., :-2, 1:-1] - 2.0 * center
        second_y = field[..., 1:-1, 2:] + field[..., 1:-1, :-2] - 2.0 * center
        mixed = 0.25 * (
            field[..., 2:, 2:] - field[..., 2:, :-2] - field[..., :-2, 2:] + field[..., :-2, :-2]
        )
        return (center, second_x, second_y, mixed)

    part_u = pieces(padded[..., 0, :, :])
    part_v = pieces(padded[..., 1, :, :])
    along_u = (
        diag_field * part_u[0]
        - 1.25 * zeta_field * part_u[1]
        - 0.25 * zeta_field * part_u[2]
        - zeta_field * part_v[3]
    )
    along_v = (
        diag_field * part_v[0]
        - 0.25 * zeta_field * part_v[1]
        - 1.25 * zeta_field * part_v[2]
        - zeta_field * part_u[3]
    )
    return jnp.stack([along_u, along_v], axis=-3)


def block_stencil(field, zeta_field, diag_field, offset):
    rows = (lax.broadcasted_iota(jnp.int32, field.shape[-2:], 0) - offset) % BS
    cols = (lax.broadcasted_iota(jnp.int32, field.shape[-2:], 1) - offset) % BS
    padded = jnp.pad(field, ((0, 0), (1, 1), (1, 1)))
    height, width = field.shape[-2:]

    def neighbour(di, dj):
        inside = jnp.ones(field.shape[-2:], jnp.bool_)
        if di:
            inside = inside & (rows != (BS - 1 if di > 0 else 0))
        if dj:
            inside = inside & (cols != (BS - 1 if dj > 0 else 0))
        window = padded[:, 1 + di : 1 + di + height, 1 + dj : 1 + dj + width]
        return jnp.where(inside, window, 0.0)

    def pieces(channel):
        center = field[channel]
        second_x = neighbour(1, 0)[channel] + neighbour(-1, 0)[channel] - 2.0 * center
        second_y = neighbour(0, 1)[channel] + neighbour(0, -1)[channel] - 2.0 * center
        mixed = 0.25 * (
            neighbour(1, 1)[channel]
            - neighbour(1, -1)[channel]
            - neighbour(-1, 1)[channel]
            + neighbour(-1, -1)[channel]
        )
        return (center, second_x, second_y, mixed)

    part_u = pieces(0)
    part_v = pieces(1)
    along_u = (
        diag_field * part_u[0]
        - 1.25 * zeta_field * part_u[1]
        - 0.25 * zeta_field * part_u[2]
        - zeta_field * part_v[3]
    )
    along_v = (
        diag_field * part_v[0]
        - 0.25 * zeta_field * part_v[1]
        - 1.25 * zeta_field * part_v[2]
        - zeta_field * part_u[3]
    )
    return jnp.stack([along_u, along_v], axis=0)


def precondition(vector, zeta_field, diag_field, diagonal_total, offset):
    iterate = vector / diagonal_total
    for relaxation in range(SWEEPS):
        iterate = (
            iterate
            + RELAX
            * (vector - block_stencil(iterate, zeta_field, diag_field, offset))
            / diagonal_total
        )
    return iterate


def widened(array, width):
    for axis, dim in (("row", 1), (COLS, 2)):
        size, length = (lax.axis_size(axis), array.shape[dim])
        up = [(i, i + 1) for i in range(size - 1)]
        down = [(j, i) for i, j in up]
        last = lax.slice_in_dim(array, length - width, length, axis=dim)
        initial = lax.slice_in_dim(array, 0, width, axis=dim)
        before = lax.ppermute(last, axis, up)
        after = lax.ppermute(initial, axis, down)
        array = jnp.concatenate([before, array, after], axis=dim)
    return array


def least_squares(h, start_norm):
    steps_count = KRYLOV
    row_list = [[h[i][j] for j in range(steps_count)] for i in range(steps_count + 1)]
    target_vec = [start_norm] + [jnp.zeros_like(start_norm) for i in range(steps_count)]
    for j in range(steps_count):
        upper = row_list[j][j]
        lower = row_list[j + 1][j]
        radius = jnp.sqrt(upper * upper + lower * lower)
        cosine = upper / radius
        sine_part = lower / radius
        first_row = [cosine * p + sine_part * q for p, q in zip(row_list[j], row_list[j + 1])]
        second_row = [-sine_part * p + cosine * q for p, q in zip(row_list[j], row_list[j + 1])]
        row_list[j], row_list[j + 1] = (first_row, second_row)
        first_val = cosine * target_vec[j] + sine_part * target_vec[j + 1]
        second_val = -sine_part * target_vec[j] + cosine * target_vec[j + 1]
        target_vec[j], target_vec[j + 1] = (first_val, second_val)
    weights_out = [None] * steps_count
    for j in range(steps_count - 1, -1, -1):
        accum = target_vec[j]
        for i in range(j + 1, steps_count):
            accum = accum - row_list[j][i] * weights_out[i]
        weights_out[j] = accum / row_list[j][j]
    return weights_out


def krylov_coefficients(gram):
    count = len(gram)

    def dot(p, q):
        total = None
        for i in range(count):
            for j in range(count):
                term = p[i] * gram[i][j] * q[j]
                total = term if total is None else total + term
        return total

    def shift(p):
        return [SHIFT * p[0]] + [x + SHIFT * y for x, y in zip(p[:-1], p[1:])]

    def scale(p, s):
        return [x * s for x in p]

    def axpy(p, s, q):
        return [x - s * y for x, y in zip(p, q)]

    one = jnp.ones_like(gram[0][0])
    zero = jnp.zeros_like(gram[0][0])
    residual = [one] + [zero] * (count - 1)
    solution = [zero] * count
    for restart in range(CYCLES):
        start_norm = jnp.sqrt(dot(residual, residual))
        basis_list = [scale(residual, 1.0 / start_norm)]
        images_list = []
        h = [[zero] * KRYLOV for _ in range(KRYLOV + 1)]
        for arnoldi in range(KRYLOV):
            images = shift(basis_list[arnoldi])
            images_list.append(images)
            products = [dot(images, vector) for vector in basis_list]
            for i in range(arnoldi + 1):
                images = axpy(images, products[i], basis_list[i])
            new_norm = jnp.sqrt(dot(images, images))
            for i in range(arnoldi + 1):
                h[i][arnoldi] = products[i]
            h[arnoldi + 1][arnoldi] = new_norm
            if arnoldi + 1 < KRYLOV:
                basis_list.append(scale(images, 1.0 / new_norm))
        weights_out = least_squares(h, start_norm)
        for arnoldi in range(KRYLOV):
            solution = [u + weights_out[arnoldi] * b for u, b in zip(solution, basis_list[arnoldi])]
            residual = axpy(residual, weights_out[arnoldi], images_list[arnoldi])
    return solution


def gram_kernel(count, *refs):
    vectors = [refs[i][...] for i in range(count)]
    out_ref = refs[count]
    shape = out_ref.shape
    rows = lax.broadcasted_iota(jnp.int32, shape, 0)
    lanes = lax.broadcasted_iota(jnp.int32, shape, 1)
    result = jnp.zeros(shape, jnp.float32)
    index = 0
    for i in range(count):
        for j in range(i, count):
            product = vectors[i] * vectors[j]
            part = jnp.sum(jnp.sum(product, axis=0, keepdims=True), axis=1, keepdims=True)
            result = jnp.where((rows == 0) & (lanes == index), part, result)
            index += 1
    out_ref[...] = result


def local_gram(krylov):
    count = len(krylov)
    flat = [k.reshape(-1, k.shape[-1]) for k in krylov]
    return pl.pallas_call(
        lambda *refs: gram_kernel(count, *refs),
        out_shape=jax.ShapeDtypeStruct((8, 128), jnp.float32),
        in_specs=[pl.BlockSpec(memory_space=pltpu.VMEM)] * count,
        out_specs=pl.BlockSpec(memory_space=pltpu.VMEM),
    )(*flat)


def coefficients_kernel(count, total_ref, out_ref):
    shape = out_ref.shape
    pairs = [(i, j) for i in range(count) for j in range(i, count)]
    gram = [[None] * count for _ in range(count)]
    for index, (i, j) in enumerate(pairs):
        value = jnp.full(shape, total_ref[0, index], jnp.float32)
        gram[i][j] = value
        gram[j][i] = value
    update = krylov_coefficients(gram)
    rows = lax.broadcasted_iota(jnp.int32, shape, 0)
    result = jnp.zeros(shape, jnp.float32)
    for k, value in enumerate(update[: count - 1]):
        result = jnp.where(rows == k, value, result)
    out_ref[...] = result


def solve_small(total, count):
    out = pl.pallas_call(
        lambda total_ref, out_ref: coefficients_kernel(count, total_ref, out_ref),
        out_shape=jax.ShapeDtypeStruct((8, 128), jnp.float32),
        in_specs=[pl.BlockSpec(memory_space=pltpu.SMEM)],
        out_specs=pl.BlockSpec(memory_space=pltpu.VMEM),
    )(total)
    column = out[:, 0]
    return [column[k] for k in range(count - 1)]


def butterfly(values, axis):
    size = lax.axis_size(axis)
    stride = 1
    while stride < size:
        values = values + lax.ppermute(values, axis, [(i, i ^ stride) for i in range(size)])
        stride *= 2
    return values


def reduce_all(values):
    return butterfly(butterfly(butterfly(values, "chip"), "row"), "grp")


def shards(
    old_velocity, surface_stress, mass_term, ocean_drag, strength, ice_mask, ocean_mask, ice_blocks
):
    tile_rows = old_velocity.shape[1]
    tile_cols = old_velocity.shape[2]
    per_row = tile_cols // BS
    tile_blocks = tile_rows // BS * per_row
    width = CYCLES * KRYLOV * (1 + SWEEPS) + 1

    is_ocean = ocean_mask.astype(jnp.float32)
    strength_part = is_ocean * ice_mask.astype(jnp.float32) * strength
    diag_tile = is_ocean * (mass_term + ocean_drag) + (1.0 - is_ocean)
    my_row = lax.axis_index("row")
    listed = ice_blocks[0]
    wanted = my_row * tile_blocks + jnp.arange(tile_blocks, dtype=jnp.int32)
    flags = jnp.any(listed[:, None] == wanted[None, :], axis=0).astype(jnp.float32)
    live_tile = jnp.repeat(
        jnp.repeat(flags.reshape(tile_rows // BS, per_row), BS, axis=0), BS, axis=1
    )
    rhs_tile = live_tile * is_ocean * (surface_stress + mass_term * old_velocity)
    fields = jnp.concatenate(
        [
            old_velocity,
            rhs_tile,
            jnp.stack([diag_tile, strength_part, live_tile, jnp.ones_like(diag_tile)]),
        ],
        axis=0,
    )
    grown = widened(fields, width)
    rhs = grown[2:4]
    diag_field = grown[4]
    live = grown[6]
    on_grid = grown[7] > 0.5

    padded = jnp.pad(grown[0:2], ((0, 0), (1, 1), (1, 1)))
    flow_u = padded[0]
    flow_v = padded[1]
    strain_xx = 0.5 * (flow_u[2:, 1:-1] - flow_u[:-2, 1:-1])
    strain_yy = 0.5 * (flow_v[1:-1, 2:] - flow_v[1:-1, :-2])
    strain_xy = 0.25 * (flow_u[1:-1, 2:] - flow_u[1:-1, :-2] + flow_v[2:, 1:-1] - flow_v[:-2, 1:-1])
    deform_sq = (
        1.25 * (strain_xx * strain_xx + strain_yy * strain_yy)
        + strain_xy * strain_xy
        + 1.5 * strain_xx * strain_yy
    )
    zeta_field = grown[5] / (2.0 * jnp.sqrt(deform_sq + DMIN_SQ))
    diagonal_total = jnp.where(on_grid, diag_field + 3.0 * zeta_field, 1.0)

    def apply_system(vector):
        return live * stencil(jnp.pad(vector, ((0, 0), (1, 1), (1, 1))), zeta_field, diag_field)

    def apply_precond(vector):
        return precondition(vector, zeta_field, diag_field, diagonal_total, width)

    def own(vector):
        return vector[:, width : width + tile_rows, width : width + tile_cols]

    krylov = [rhs]
    directions = []
    for step in range(CYCLES * KRYLOV):
        directions.append(apply_precond(krylov[-1]))
        krylov.append(apply_system(directions[-1]) - SHIFT * krylov[-1])
    total = reduce_all(local_gram([own(k) for k in krylov]))
    update = solve_small(total, len(krylov))
    solution = update[0] * own(directions[0])
    for i in range(1, len(directions)):
        solution = solution + update[i] * own(directions[i])
    return solution


def solution(mesh):
    return jax.shard_map(
        shards,
        mesh=mesh,
        in_specs=(
            P(None, "row", COLS),
            P(None, "row", COLS),
            P("row", COLS),
            P("row", COLS),
            P("row", COLS),
            P("row", COLS),
            P("row", COLS),
            P(COLS, None),
        ),
        out_specs=P(None, "row", COLS),
        check_vma=False,
    )
```

```python
import jax
import jax.numpy as jnp
from jax import lax
from jax.experimental import pallas as pl
from jax.experimental.pallas import tpu as pltpu
from jax.sharding import PartitionSpec as P

BS = 128
KRYLOV = 2
CYCLES = 2
SWEEPS = 2


RELAX = 0.8
DMIN_SQ = 0.25
SHIFT = 1.0

COLS = ("chip", "grp")


def combine(center, second_x, second_y, mixed, zeta_field, diag_field):
    weight_x = jnp.array([1.25, 0.25], jnp.float32)[:, None, None]
    weight_y = jnp.array([0.25, 1.25], jnp.float32)[:, None, None]
    return (
        diag_field * center
        - weight_x * zeta_field * second_x
        - weight_y * zeta_field * second_y
        - zeta_field * mixed[::-1]
    )


def stencil(padded, zeta_field, diag_field):
    center = padded[..., 1:-1, 1:-1]
    second_x = padded[..., 2:, 1:-1] + padded[..., :-2, 1:-1] - 2.0 * center
    second_y = padded[..., 1:-1, 2:] + padded[..., 1:-1, :-2] - 2.0 * center
    mixed = 0.25 * (
        padded[..., 2:, 2:] - padded[..., 2:, :-2] - padded[..., :-2, 2:] + padded[..., :-2, :-2]
    )
    return combine(center, second_x, second_y, mixed, zeta_field, diag_field)


def block_stencil(field, zeta_field, diag_field, offset):
    rows = (lax.broadcasted_iota(jnp.int32, field.shape[-2:], 0) - offset) % BS
    cols = (lax.broadcasted_iota(jnp.int32, field.shape[-2:], 1) - offset) % BS
    padded = jnp.pad(field, ((0, 0), (1, 1), (1, 1)))
    height, width = field.shape[-2:]

    def neighbour(di, dj):
        inside = jnp.ones(field.shape[-2:], jnp.bool_)
        if di:
            inside = inside & (rows != (BS - 1 if di > 0 else 0))
        if dj:
            inside = inside & (cols != (BS - 1 if dj > 0 else 0))
        window = padded[:, 1 + di : 1 + di + height, 1 + dj : 1 + dj + width]
        return jnp.where(inside, window, 0.0)

    center = field
    second_x = neighbour(1, 0) + neighbour(-1, 0) - 2.0 * center
    second_y = neighbour(0, 1) + neighbour(0, -1) - 2.0 * center
    mixed = 0.25 * (neighbour(1, 1) - neighbour(1, -1) - neighbour(-1, 1) + neighbour(-1, -1))
    return combine(center, second_x, second_y, mixed, zeta_field, diag_field)


def precondition(vector, zeta_field, diag_field, diagonal_total, offset):
    iterate = vector / diagonal_total
    for relaxation in range(SWEEPS):
        iterate = (
            iterate
            + RELAX
            * (vector - block_stencil(iterate, zeta_field, diag_field, offset))
            / diagonal_total
        )
    return iterate


def widened(array, width):
    for axis, dim in (("row", 1), (COLS, 2)):
        size, length = (lax.axis_size(axis), array.shape[dim])
        up = [(i, i + 1) for i in range(size - 1)]
        down = [(j, i) for i, j in up]
        last = lax.slice_in_dim(array, length - width, length, axis=dim)
        initial = lax.slice_in_dim(array, 0, width, axis=dim)
        before = lax.ppermute(last, axis, up)
        after = lax.ppermute(initial, axis, down)
        array = jnp.concatenate([before, array, after], axis=dim)
    return array


def least_squares(h, start_norm):
    steps_count = KRYLOV
    row_list = [[h[i][j] for j in range(steps_count)] for i in range(steps_count + 1)]
    target_vec = [start_norm] + [jnp.zeros_like(start_norm) for i in range(steps_count)]
    for j in range(steps_count):
        upper = row_list[j][j]
        lower = row_list[j + 1][j]
        radius = jnp.sqrt(upper * upper + lower * lower)
        cosine = upper / radius
        sine_part = lower / radius
        first_row = [cosine * p + sine_part * q for p, q in zip(row_list[j], row_list[j + 1])]
        second_row = [-sine_part * p + cosine * q for p, q in zip(row_list[j], row_list[j + 1])]
        row_list[j], row_list[j + 1] = (first_row, second_row)
        first_val = cosine * target_vec[j] + sine_part * target_vec[j + 1]
        second_val = -sine_part * target_vec[j] + cosine * target_vec[j + 1]
        target_vec[j], target_vec[j + 1] = (first_val, second_val)
    weights_out = [None] * steps_count
    for j in range(steps_count - 1, -1, -1):
        accum = target_vec[j]
        for i in range(j + 1, steps_count):
            accum = accum - row_list[j][i] * weights_out[i]
        weights_out[j] = accum / row_list[j][j]
    return weights_out


def krylov_coefficients(gram):
    count = len(gram)

    def dot(p, q):
        total = None
        for i in range(count):
            for j in range(count):
                term = p[i] * gram[i][j] * q[j]
                total = term if total is None else total + term
        return total

    def shift(p):
        return [SHIFT * p[0]] + [x + SHIFT * y for x, y in zip(p[:-1], p[1:])]

    def scale(p, s):
        return [x * s for x in p]

    def axpy(p, s, q):
        return [x - s * y for x, y in zip(p, q)]

    one = jnp.ones_like(gram[0][0])
    zero = jnp.zeros_like(gram[0][0])
    residual = [one] + [zero] * (count - 1)
    solution = [zero] * count
    for restart in range(CYCLES):
        start_norm = jnp.sqrt(dot(residual, residual))
        basis_list = [scale(residual, 1.0 / start_norm)]
        images_list = []
        h = [[zero] * KRYLOV for _ in range(KRYLOV + 1)]
        for arnoldi in range(KRYLOV):
            images = shift(basis_list[arnoldi])
            images_list.append(images)
            products = [dot(images, vector) for vector in basis_list]
            for i in range(arnoldi + 1):
                images = axpy(images, products[i], basis_list[i])
            new_norm = jnp.sqrt(dot(images, images))
            for i in range(arnoldi + 1):
                h[i][arnoldi] = products[i]
            h[arnoldi + 1][arnoldi] = new_norm
            if arnoldi + 1 < KRYLOV:
                basis_list.append(scale(images, 1.0 / new_norm))
        weights_out = least_squares(h, start_norm)
        for arnoldi in range(KRYLOV):
            solution = [u + weights_out[arnoldi] * b for u, b in zip(solution, basis_list[arnoldi])]
            residual = axpy(residual, weights_out[arnoldi], images_list[arnoldi])
    return solution


def gram_kernel(count, width, tile_rows, tile_cols, *refs):
    vectors = [refs[i][...] for i in range(count)]
    out_ref = refs[count]
    extent = vectors[0].shape[-2:]
    cell_rows = lax.broadcasted_iota(jnp.int32, extent, 0)
    cell_cols = lax.broadcasted_iota(jnp.int32, extent, 1)
    own = (
        (cell_rows >= width)
        & (cell_rows < width + tile_rows)
        & (cell_cols >= width)
        & (cell_cols < width + tile_cols)
    )
    vectors = [jnp.where(own, v, 0.0) for v in vectors]
    shape = out_ref.shape
    rows = lax.broadcasted_iota(jnp.int32, shape, 0)
    lanes = lax.broadcasted_iota(jnp.int32, shape, 1)
    result = jnp.zeros(shape, jnp.float32)
    index = 0
    for i in range(count):
        for j in range(i, count):
            product = jnp.sum(vectors[i] * vectors[j], axis=0)
            part = jnp.sum(jnp.sum(product, axis=0, keepdims=True), axis=1, keepdims=True)
            result = jnp.where((rows == 0) & (lanes == index), part, result)
            index += 1
    out_ref[...] = result


def local_gram(krylov, width, tile_rows, tile_cols):
    count = len(krylov)
    return pl.pallas_call(
        lambda *refs: gram_kernel(count, width, tile_rows, tile_cols, *refs),
        out_shape=jax.ShapeDtypeStruct((8, 128), jnp.float32),
        in_specs=[pl.BlockSpec(memory_space=pltpu.VMEM)] * count,
        out_specs=pl.BlockSpec(memory_space=pltpu.VMEM),
    )(*krylov)


def coefficients_kernel(count, total_ref, out_ref):
    shape = out_ref.shape
    pairs = [(i, j) for i in range(count) for j in range(i, count)]
    gram = [[None] * count for _ in range(count)]
    for index, (i, j) in enumerate(pairs):
        value = jnp.full(shape, total_ref[0, index], jnp.float32)
        gram[i][j] = value
        gram[j][i] = value
    update = krylov_coefficients(gram)
    rows = lax.broadcasted_iota(jnp.int32, shape, 0)
    result = jnp.zeros(shape, jnp.float32)
    for k, value in enumerate(update[: count - 1]):
        result = jnp.where(rows == k, value, result)
    out_ref[...] = result


def solve_small(total, count):
    out = pl.pallas_call(
        lambda total_ref, out_ref: coefficients_kernel(count, total_ref, out_ref),
        out_shape=jax.ShapeDtypeStruct((8, 128), jnp.float32),
        in_specs=[pl.BlockSpec(memory_space=pltpu.SMEM)],
        out_specs=pl.BlockSpec(memory_space=pltpu.VMEM),
    )(total)
    column = out[:, 0]
    return [column[k] for k in range(count - 1)]


def butterfly(values, axis):
    size = lax.axis_size(axis)
    stride = 1
    while stride < size:
        values = values + lax.ppermute(values, axis, [(i, i ^ stride) for i in range(size)])
        stride *= 2
    return values


def reduce_all(values):
    return butterfly(butterfly(butterfly(values, "chip"), "row"), "grp")


def shards(
    old_velocity, surface_stress, mass_term, ocean_drag, strength, ice_mask, ocean_mask, ice_blocks
):
    tile_rows = old_velocity.shape[1]
    tile_cols = old_velocity.shape[2]
    per_row = tile_cols // BS
    tile_blocks = tile_rows // BS * per_row
    width = CYCLES * KRYLOV * (1 + SWEEPS) + 1

    is_ocean = ocean_mask.astype(jnp.float32)
    strength_part = is_ocean * ice_mask.astype(jnp.float32) * strength
    diag_tile = is_ocean * (mass_term + ocean_drag) + (1.0 - is_ocean)
    my_row = lax.axis_index("row")
    listed = ice_blocks[0]
    wanted = my_row * tile_blocks + jnp.arange(tile_blocks, dtype=jnp.int32)
    flags = jnp.any(listed[:, None] == wanted[None, :], axis=0).astype(jnp.float32)
    live_tile = jnp.repeat(
        jnp.repeat(flags.reshape(tile_rows // BS, per_row), BS, axis=0), BS, axis=1
    )
    rhs_tile = live_tile * is_ocean * (surface_stress + mass_term * old_velocity)
    fields = jnp.concatenate(
        [
            old_velocity,
            rhs_tile,
            jnp.stack([diag_tile, strength_part, live_tile, jnp.ones_like(diag_tile)]),
        ],
        axis=0,
    )
    grown = widened(fields, width)
    rhs = grown[2:4]
    diag_field = grown[4]
    live = grown[6]
    on_grid = grown[7] > 0.5

    padded = jnp.pad(grown[0:2], ((0, 0), (1, 1), (1, 1)))
    flow_u = padded[0]
    flow_v = padded[1]
    strain_xx = 0.5 * (flow_u[2:, 1:-1] - flow_u[:-2, 1:-1])
    strain_yy = 0.5 * (flow_v[1:-1, 2:] - flow_v[1:-1, :-2])
    strain_xy = 0.25 * (flow_u[1:-1, 2:] - flow_u[1:-1, :-2] + flow_v[2:, 1:-1] - flow_v[:-2, 1:-1])
    deform_sq = (
        1.25 * (strain_xx * strain_xx + strain_yy * strain_yy)
        + strain_xy * strain_xy
        + 1.5 * strain_xx * strain_yy
    )
    zeta_field = grown[5] / (2.0 * jnp.sqrt(deform_sq + DMIN_SQ))
    diagonal_total = jnp.where(on_grid, diag_field + 3.0 * zeta_field, 1.0)

    def apply_system(vector):
        return live * stencil(jnp.pad(vector, ((0, 0), (1, 1), (1, 1))), zeta_field, diag_field)

    def apply_precond(vector):
        return precondition(vector, zeta_field, diag_field, diagonal_total, width)

    def own(vector):
        return vector[:, width : width + tile_rows, width : width + tile_cols]

    krylov = [rhs]
    directions = []
    for step in range(CYCLES * KRYLOV):
        directions.append(apply_precond(krylov[-1]))
        krylov.append(apply_system(directions[-1]) - SHIFT * krylov[-1])
    total = reduce_all(local_gram(krylov, width, tile_rows, tile_cols))
    update = solve_small(total, len(krylov))
    solution = update[0] * own(directions[0])
    for i in range(1, len(directions)):
        solution = solution + update[i] * own(directions[i])
    return solution


def solution(mesh):
    return jax.shard_map(
        shards,
        mesh=mesh,
        in_specs=(
            P(None, "row", COLS),
            P(None, "row", COLS),
            P("row", COLS),
            P("row", COLS),
            P("row", COLS),
            P("row", COLS),
            P("row", COLS),
            P(COLS, None),
        ),
        out_specs=P(None, "row", COLS),
        check_vma=False,
    )
```

```python
import jax
import jax.numpy as jnp
from jax import lax
from jax.experimental import pallas as pl
from jax.experimental.pallas import tpu as pltpu
from jax.sharding import PartitionSpec as P

BS = 128
KRYLOV = 2
CYCLES = 2
SWEEPS = 2


RELAX = 0.8
DMIN_SQ = 0.25
SHIFT = 1.0

COLS = ("chip", "grp")


def combine(center, second_x, second_y, mixed, zeta_field, diag_field):
    weight_x = jnp.array([1.25, 0.25], jnp.float32)[:, None, None]
    weight_y = jnp.array([0.25, 1.25], jnp.float32)[:, None, None]
    return (
        diag_field * center
        - weight_x * zeta_field * second_x
        - weight_y * zeta_field * second_y
        - zeta_field * mixed[::-1]
    )


def stencil(padded, zeta_field, diag_field):
    center = padded[..., 1:-1, 1:-1]
    second_x = padded[..., 2:, 1:-1] + padded[..., :-2, 1:-1] - 2.0 * center
    second_y = padded[..., 1:-1, 2:] + padded[..., 1:-1, :-2] - 2.0 * center
    mixed = 0.25 * (
        padded[..., 2:, 2:] - padded[..., 2:, :-2] - padded[..., :-2, 2:] + padded[..., :-2, :-2]
    )
    return combine(center, second_x, second_y, mixed, zeta_field, diag_field)


def block_stencil(field, zeta_field, diag_field, offset):
    rows = (lax.broadcasted_iota(jnp.int32, field.shape[-2:], 0) - offset) % BS
    cols = (lax.broadcasted_iota(jnp.int32, field.shape[-2:], 1) - offset) % BS
    padded = jnp.pad(field, ((0, 0), (1, 1), (1, 1)))
    height, width = field.shape[-2:]

    def neighbour(di, dj):
        inside = jnp.ones(field.shape[-2:], jnp.bool_)
        if di:
            inside = inside & (rows != (BS - 1 if di > 0 else 0))
        if dj:
            inside = inside & (cols != (BS - 1 if dj > 0 else 0))
        window = padded[:, 1 + di : 1 + di + height, 1 + dj : 1 + dj + width]
        return jnp.where(inside, window, 0.0)

    center = field
    second_x = neighbour(1, 0) + neighbour(-1, 0) - 2.0 * center
    second_y = neighbour(0, 1) + neighbour(0, -1) - 2.0 * center
    mixed = 0.25 * (neighbour(1, 1) - neighbour(1, -1) - neighbour(-1, 1) + neighbour(-1, -1))
    return combine(center, second_x, second_y, mixed, zeta_field, diag_field)


def precondition(vector, zeta_field, diag_field, diagonal_total, offset):
    iterate = vector / diagonal_total
    for relaxation in range(SWEEPS):
        iterate = (
            iterate
            + RELAX
            * (vector - block_stencil(iterate, zeta_field, diag_field, offset))
            / diagonal_total
        )
    return iterate


def widened(array, width):
    rows, cols = (lax.axis_size("row"), lax.axis_size(COLS))
    group = lax.axis_size("grp")
    every = ("chip", "row", "grp")

    def linear(r, c):
        return (c // group) * (rows * group) + r * group + c % group

    def moved(piece, dr, dc):
        pairs = [
            (linear(r, c), linear(r + dr, c + dc))
            for r in range(rows)
            for c in range(cols)
            if 0 <= r + dr < rows and 0 <= c + dc < cols
        ]
        return lax.ppermute(piece, every, pairs)

    height, length = array.shape[1], array.shape[2]
    top, bottom = array[:, :width], array[:, height - width :]
    left, right = array[:, :, :width], array[:, :, length - width :]
    above = moved(bottom, 1, 0)
    below = moved(top, -1, 0)
    before = moved(right, 0, 1)
    after = moved(left, 0, -1)
    corner_tl = moved(bottom[:, :, length - width :], 1, 1)
    corner_tr = moved(bottom[:, :, :width], 1, -1)
    corner_bl = moved(top[:, :, length - width :], -1, 1)
    corner_br = moved(top[:, :, :width], -1, -1)
    upper = jnp.concatenate([corner_tl, above, corner_tr], axis=2)
    middle = jnp.concatenate([before, array, after], axis=2)
    lower = jnp.concatenate([corner_bl, below, corner_br], axis=2)
    return jnp.concatenate([upper, middle, lower], axis=1)


def least_squares(h, start_norm):
    steps_count = KRYLOV
    row_list = [[h[i][j] for j in range(steps_count)] for i in range(steps_count + 1)]
    target_vec = [start_norm] + [jnp.zeros_like(start_norm) for i in range(steps_count)]
    for j in range(steps_count):
        upper = row_list[j][j]
        lower = row_list[j + 1][j]
        radius = jnp.sqrt(upper * upper + lower * lower)
        cosine = upper / radius
        sine_part = lower / radius
        first_row = [cosine * p + sine_part * q for p, q in zip(row_list[j], row_list[j + 1])]
        second_row = [-sine_part * p + cosine * q for p, q in zip(row_list[j], row_list[j + 1])]
        row_list[j], row_list[j + 1] = (first_row, second_row)
        first_val = cosine * target_vec[j] + sine_part * target_vec[j + 1]
        second_val = -sine_part * target_vec[j] + cosine * target_vec[j + 1]
        target_vec[j], target_vec[j + 1] = (first_val, second_val)
    weights_out = [None] * steps_count
    for j in range(steps_count - 1, -1, -1):
        accum = target_vec[j]
        for i in range(j + 1, steps_count):
            accum = accum - row_list[j][i] * weights_out[i]
        weights_out[j] = accum / row_list[j][j]
    return weights_out


def krylov_coefficients(gram):
    count = len(gram)

    def dot(p, q):
        total = None
        for i in range(count):
            for j in range(count):
                term = p[i] * gram[i][j] * q[j]
                total = term if total is None else total + term
        return total

    def shift(p):
        return [SHIFT * p[0]] + [x + SHIFT * y for x, y in zip(p[:-1], p[1:])]

    def scale(p, s):
        return [x * s for x in p]

    def axpy(p, s, q):
        return [x - s * y for x, y in zip(p, q)]

    one = jnp.ones_like(gram[0][0])
    zero = jnp.zeros_like(gram[0][0])
    residual = [one] + [zero] * (count - 1)
    solution = [zero] * count
    for restart in range(CYCLES):
        start_norm = jnp.sqrt(dot(residual, residual))
        basis_list = [scale(residual, 1.0 / start_norm)]
        images_list = []
        h = [[zero] * KRYLOV for _ in range(KRYLOV + 1)]
        for arnoldi in range(KRYLOV):
            images = shift(basis_list[arnoldi])
            images_list.append(images)
            products = [dot(images, vector) for vector in basis_list]
            for i in range(arnoldi + 1):
                images = axpy(images, products[i], basis_list[i])
            new_norm = jnp.sqrt(dot(images, images))
            for i in range(arnoldi + 1):
                h[i][arnoldi] = products[i]
            h[arnoldi + 1][arnoldi] = new_norm
            if arnoldi + 1 < KRYLOV:
                basis_list.append(scale(images, 1.0 / new_norm))
        weights_out = least_squares(h, start_norm)
        for arnoldi in range(KRYLOV):
            solution = [u + weights_out[arnoldi] * b for u, b in zip(solution, basis_list[arnoldi])]
            residual = axpy(residual, weights_out[arnoldi], images_list[arnoldi])
    return solution


def gram_kernel(count, width, tile_rows, tile_cols, *refs):
    vectors = [refs[i][...] for i in range(count)]
    out_ref = refs[count]
    extent = vectors[0].shape[-2:]
    cell_rows = lax.broadcasted_iota(jnp.int32, extent, 0)
    cell_cols = lax.broadcasted_iota(jnp.int32, extent, 1)
    own = (
        (cell_rows >= width)
        & (cell_rows < width + tile_rows)
        & (cell_cols >= width)
        & (cell_cols < width + tile_cols)
    )
    vectors = [jnp.where(own, v, 0.0) for v in vectors]
    shape = out_ref.shape
    rows = lax.broadcasted_iota(jnp.int32, shape, 0)
    lanes = lax.broadcasted_iota(jnp.int32, shape, 1)
    result = jnp.zeros(shape, jnp.float32)
    index = 0
    for i in range(count):
        for j in range(i, count):
            product = jnp.sum(vectors[i] * vectors[j], axis=0)
            part = jnp.sum(jnp.sum(product, axis=0, keepdims=True), axis=1, keepdims=True)
            result = jnp.where((rows == 0) & (lanes == index), part, result)
            index += 1
    out_ref[...] = result


def local_gram(krylov, width, tile_rows, tile_cols):
    count = len(krylov)
    return pl.pallas_call(
        lambda *refs: gram_kernel(count, width, tile_rows, tile_cols, *refs),
        out_shape=jax.ShapeDtypeStruct((8, 128), jnp.float32),
        in_specs=[pl.BlockSpec(memory_space=pltpu.VMEM)] * count,
        out_specs=pl.BlockSpec(memory_space=pltpu.VMEM),
    )(*krylov)


def coefficients_kernel(count, total_ref, out_ref):
    shape = out_ref.shape
    pairs = [(i, j) for i in range(count) for j in range(i, count)]
    gram = [[None] * count for _ in range(count)]
    for index, (i, j) in enumerate(pairs):
        value = jnp.full(shape, total_ref[0, index], jnp.float32)
        gram[i][j] = value
        gram[j][i] = value
    update = krylov_coefficients(gram)
    rows = lax.broadcasted_iota(jnp.int32, shape, 0)
    result = jnp.zeros(shape, jnp.float32)
    for k, value in enumerate(update[: count - 1]):
        result = jnp.where(rows == k, value, result)
    out_ref[...] = result


def solve_small(total, count):
    out = pl.pallas_call(
        lambda total_ref, out_ref: coefficients_kernel(count, total_ref, out_ref),
        out_shape=jax.ShapeDtypeStruct((8, 128), jnp.float32),
        in_specs=[pl.BlockSpec(memory_space=pltpu.SMEM)],
        out_specs=pl.BlockSpec(memory_space=pltpu.VMEM),
    )(total)
    column = out[:, 0]
    return [column[k] for k in range(count - 1)]


def butterfly(values, axis):
    size = lax.axis_size(axis)
    stride = 1
    while stride < size:
        values = values + lax.ppermute(values, axis, [(i, i ^ stride) for i in range(size)])
        stride *= 2
    return values


def reduce_all(values):
    return butterfly(butterfly(lax.psum(values, "chip"), "row"), "grp")


def shards(
    old_velocity, surface_stress, mass_term, ocean_drag, strength, ice_mask, ocean_mask, ice_blocks
):
    tile_rows = old_velocity.shape[1]
    tile_cols = old_velocity.shape[2]
    per_row = tile_cols // BS
    tile_blocks = tile_rows // BS * per_row
    width = CYCLES * KRYLOV * (1 + SWEEPS) + 1

    is_ocean = ocean_mask.astype(jnp.float32)
    strength_part = is_ocean * ice_mask.astype(jnp.float32) * strength
    diag_tile = is_ocean * (mass_term + ocean_drag) + (1.0 - is_ocean)
    my_row = lax.axis_index("row")
    listed = ice_blocks[0]
    wanted = my_row * tile_blocks + jnp.arange(tile_blocks, dtype=jnp.int32)
    flags = jnp.any(listed[:, None] == wanted[None, :], axis=0).astype(jnp.float32)
    live_tile = jnp.repeat(
        jnp.repeat(flags.reshape(tile_rows // BS, per_row), BS, axis=0), BS, axis=1
    )
    rhs_tile = live_tile * is_ocean * (surface_stress + mass_term * old_velocity)
    fields = jnp.concatenate(
        [
            old_velocity,
            rhs_tile,
            jnp.stack([diag_tile, strength_part, live_tile, jnp.ones_like(diag_tile)]),
        ],
        axis=0,
    )
    grown = widened(fields, width)
    rhs = grown[2:4]
    diag_field = grown[4]
    live = grown[6]
    on_grid = grown[7] > 0.5

    padded = jnp.pad(grown[0:2], ((0, 0), (1, 1), (1, 1)))
    flow_u = padded[0]
    flow_v = padded[1]
    strain_xx = 0.5 * (flow_u[2:, 1:-1] - flow_u[:-2, 1:-1])
    strain_yy = 0.5 * (flow_v[1:-1, 2:] - flow_v[1:-1, :-2])
    strain_xy = 0.25 * (flow_u[1:-1, 2:] - flow_u[1:-1, :-2] + flow_v[2:, 1:-1] - flow_v[:-2, 1:-1])
    deform_sq = (
        1.25 * (strain_xx * strain_xx + strain_yy * strain_yy)
        + strain_xy * strain_xy
        + 1.5 * strain_xx * strain_yy
    )
    zeta_field = grown[5] / (2.0 * jnp.sqrt(deform_sq + DMIN_SQ))
    diagonal_total = jnp.where(on_grid, diag_field + 3.0 * zeta_field, 1.0)

    def apply_system(vector):
        return live * stencil(jnp.pad(vector, ((0, 0), (1, 1), (1, 1))), zeta_field, diag_field)

    def apply_precond(vector):
        return precondition(vector, zeta_field, diag_field, diagonal_total, width)

    def own(vector):
        return vector[:, width : width + tile_rows, width : width + tile_cols]

    krylov = [rhs]
    directions = []
    for step in range(CYCLES * KRYLOV):
        directions.append(apply_precond(krylov[-1]))
        krylov.append(apply_system(directions[-1]) - SHIFT * krylov[-1])
    total = reduce_all(local_gram(krylov, width, tile_rows, tile_cols))
    update = solve_small(total, len(krylov))
    solution = update[0] * own(directions[0])
    for i in range(1, len(directions)):
        solution = solution + update[i] * own(directions[i])
    return solution


def solution(mesh):
    return jax.shard_map(
        shards,
        mesh=mesh,
        in_specs=(
            P(None, "row", COLS),
            P(None, "row", COLS),
            P("row", COLS),
            P("row", COLS),
            P("row", COLS),
            P("row", COLS),
            P("row", COLS),
            P(COLS, None),
        ),
        out_specs=P(None, "row", COLS),
        check_vma=False,
    )
```

```python
import jax
import jax.numpy as jnp
from jax import lax
from jax.experimental import pallas as pl
from jax.experimental.pallas import tpu as pltpu
from jax.sharding import PartitionSpec as P

BS = 128
KRYLOV = 2
CYCLES = 2
SWEEPS = 2


RELAX = 0.8
DMIN_SQ = 0.25
SHIFT = 1.0

COLS = ("chip", "grp")


def combine(center, second_x, second_y, mixed, zeta_field, diag_field):
    weight_x = jnp.array([1.25, 0.25], jnp.float32)[:, None, None]
    weight_y = jnp.array([0.25, 1.25], jnp.float32)[:, None, None]
    return (
        diag_field * center
        - weight_x * zeta_field * second_x
        - weight_y * zeta_field * second_y
        - zeta_field * mixed[::-1]
    )


def stencil(padded, zeta_field, diag_field):
    center = padded[..., 1:-1, 1:-1]
    second_x = padded[..., 2:, 1:-1] + padded[..., :-2, 1:-1] - 2.0 * center
    second_y = padded[..., 1:-1, 2:] + padded[..., 1:-1, :-2] - 2.0 * center
    mixed = 0.25 * (
        padded[..., 2:, 2:] - padded[..., 2:, :-2] - padded[..., :-2, 2:] + padded[..., :-2, :-2]
    )
    return combine(center, second_x, second_y, mixed, zeta_field, diag_field)


def block_stencil(field, zeta_field, diag_field, offset):
    rows = (lax.broadcasted_iota(jnp.int32, field.shape[-2:], 0) - offset) % BS
    cols = (lax.broadcasted_iota(jnp.int32, field.shape[-2:], 1) - offset) % BS
    padded = jnp.pad(field, ((0, 0), (1, 1), (1, 1)))
    height, width = field.shape[-2:]

    def neighbour(di, dj):
        inside = jnp.ones(field.shape[-2:], jnp.bool_)
        if di:
            inside = inside & (rows != (BS - 1 if di > 0 else 0))
        if dj:
            inside = inside & (cols != (BS - 1 if dj > 0 else 0))
        window = padded[:, 1 + di : 1 + di + height, 1 + dj : 1 + dj + width]
        return jnp.where(inside, window, 0.0)

    center = field
    second_x = neighbour(1, 0) + neighbour(-1, 0) - 2.0 * center
    second_y = neighbour(0, 1) + neighbour(0, -1) - 2.0 * center
    mixed = 0.25 * (neighbour(1, 1) - neighbour(1, -1) - neighbour(-1, 1) + neighbour(-1, -1))
    return combine(center, second_x, second_y, mixed, zeta_field, diag_field)


def precondition(vector, zeta_field, diag_field, diagonal_total, offset):
    iterate = vector / diagonal_total
    for relaxation in range(SWEEPS):
        iterate = (
            iterate
            + RELAX
            * (vector - block_stencil(iterate, zeta_field, diag_field, offset))
            / diagonal_total
        )
    return iterate


def widened(array, width):
    for axis, dim in (("row", 1), (COLS, 2)):
        size, length = (lax.axis_size(axis), array.shape[dim])
        up = [(i, i + 1) for i in range(size - 1)]
        down = [(j, i) for i, j in up]
        last = lax.slice_in_dim(array, length - width, length, axis=dim)
        initial = lax.slice_in_dim(array, 0, width, axis=dim)
        before = lax.ppermute(last, axis, up)
        after = lax.ppermute(initial, axis, down)
        array = jnp.concatenate([before, array, after], axis=dim)
    return array


def least_squares(h, start_norm):
    steps_count = KRYLOV
    row_list = [[h[i][j] for j in range(steps_count)] for i in range(steps_count + 1)]
    target_vec = [start_norm] + [jnp.zeros_like(start_norm) for i in range(steps_count)]
    for j in range(steps_count):
        upper = row_list[j][j]
        lower = row_list[j + 1][j]
        radius = jnp.sqrt(upper * upper + lower * lower)
        cosine = upper / radius
        sine_part = lower / radius
        first_row = [cosine * p + sine_part * q for p, q in zip(row_list[j], row_list[j + 1])]
        second_row = [-sine_part * p + cosine * q for p, q in zip(row_list[j], row_list[j + 1])]
        row_list[j], row_list[j + 1] = (first_row, second_row)
        first_val = cosine * target_vec[j] + sine_part * target_vec[j + 1]
        second_val = -sine_part * target_vec[j] + cosine * target_vec[j + 1]
        target_vec[j], target_vec[j + 1] = (first_val, second_val)
    weights_out = [None] * steps_count
    for j in range(steps_count - 1, -1, -1):
        accum = target_vec[j]
        for i in range(j + 1, steps_count):
            accum = accum - row_list[j][i] * weights_out[i]
        weights_out[j] = accum / row_list[j][j]
    return weights_out


def krylov_coefficients(gram):
    count = len(gram)

    def dot(p, q):
        total = None
        for i in range(count):
            for j in range(count):
                term = p[i] * gram[i][j] * q[j]
                total = term if total is None else total + term
        return total

    def shift(p):
        return [SHIFT * p[0]] + [x + SHIFT * y for x, y in zip(p[:-1], p[1:])]

    def scale(p, s):
        return [x * s for x in p]

    def axpy(p, s, q):
        return [x - s * y for x, y in zip(p, q)]

    one = jnp.ones_like(gram[0][0])
    zero = jnp.zeros_like(gram[0][0])
    residual = [one] + [zero] * (count - 1)
    solution = [zero] * count
    for restart in range(CYCLES):
        start_norm = jnp.sqrt(dot(residual, residual))
        basis_list = [scale(residual, 1.0 / start_norm)]
        images_list = []
        h = [[zero] * KRYLOV for _ in range(KRYLOV + 1)]
        for arnoldi in range(KRYLOV):
            images = shift(basis_list[arnoldi])
            images_list.append(images)
            products = [dot(images, vector) for vector in basis_list]
            for i in range(arnoldi + 1):
                images = axpy(images, products[i], basis_list[i])
            new_norm = jnp.sqrt(dot(images, images))
            for i in range(arnoldi + 1):
                h[i][arnoldi] = products[i]
            h[arnoldi + 1][arnoldi] = new_norm
            if arnoldi + 1 < KRYLOV:
                basis_list.append(scale(images, 1.0 / new_norm))
        weights_out = least_squares(h, start_norm)
        for arnoldi in range(KRYLOV):
            solution = [u + weights_out[arnoldi] * b for u, b in zip(solution, basis_list[arnoldi])]
            residual = axpy(residual, weights_out[arnoldi], images_list[arnoldi])
    return solution


def gram_kernel(steps, width, tile_rows, tile_cols, first_ref, rest_ref, out_ref):
    vectors = [first_ref[...]] + [rest_ref[i] for i in range(steps)]
    count = len(vectors)
    extent = vectors[0].shape[-2:]
    cell_rows = lax.broadcasted_iota(jnp.int32, extent, 0)
    cell_cols = lax.broadcasted_iota(jnp.int32, extent, 1)
    own = (
        (cell_rows >= width)
        & (cell_rows < width + tile_rows)
        & (cell_cols >= width)
        & (cell_cols < width + tile_cols)
    )
    vectors = [jnp.where(own, v, 0.0) for v in vectors]
    shape = out_ref.shape
    rows = lax.broadcasted_iota(jnp.int32, shape, 0)
    lanes = lax.broadcasted_iota(jnp.int32, shape, 1)
    result = jnp.zeros(shape, jnp.float32)
    index = 0
    for i in range(count):
        for j in range(i, count):
            product = jnp.sum(vectors[i] * vectors[j], axis=0)
            part = jnp.sum(jnp.sum(product, axis=0, keepdims=True), axis=1, keepdims=True)
            result = jnp.where((rows == 0) & (lanes == index), part, result)
            index += 1
    out_ref[...] = result


def local_gram(first, rest, width, tile_rows, tile_cols):
    steps = rest.shape[0]
    return pl.pallas_call(
        lambda first_ref, rest_ref, out_ref: gram_kernel(
            steps, width, tile_rows, tile_cols, first_ref, rest_ref, out_ref
        ),
        out_shape=jax.ShapeDtypeStruct((8, 128), jnp.float32),
        in_specs=[pl.BlockSpec(memory_space=pltpu.VMEM)] * 2,
        out_specs=pl.BlockSpec(memory_space=pltpu.VMEM),
    )(first, rest)


def coefficients_kernel(count, total_ref, out_ref):
    shape = out_ref.shape
    pairs = [(i, j) for i in range(count) for j in range(i, count)]
    gram = [[None] * count for _ in range(count)]
    for index, (i, j) in enumerate(pairs):
        value = jnp.full(shape, total_ref[0, index], jnp.float32)
        gram[i][j] = value
        gram[j][i] = value
    update = krylov_coefficients(gram)
    rows = lax.broadcasted_iota(jnp.int32, shape, 0)
    result = jnp.zeros(shape, jnp.float32)
    for k, value in enumerate(update[: count - 1]):
        result = jnp.where(rows == k, value, result)
    out_ref[...] = result


def solve_small(total, count):
    out = pl.pallas_call(
        lambda total_ref, out_ref: coefficients_kernel(count, total_ref, out_ref),
        out_shape=jax.ShapeDtypeStruct((8, 128), jnp.float32),
        in_specs=[pl.BlockSpec(memory_space=pltpu.SMEM)],
        out_specs=pl.BlockSpec(memory_space=pltpu.VMEM),
    )(total)
    column = out[:, 0]
    return [column[k] for k in range(count - 1)]


def butterfly(values, axis):
    size = lax.axis_size(axis)
    stride = 1
    while stride < size:
        values = values + lax.ppermute(values, axis, [(i, i ^ stride) for i in range(size)])
        stride *= 2
    return values


def reduce_all(values):
    return butterfly(butterfly(butterfly(values, "chip"), "row"), "grp")


def shards(
    old_velocity, surface_stress, mass_term, ocean_drag, strength, ice_mask, ocean_mask, ice_blocks
):
    tile_rows = old_velocity.shape[1]
    tile_cols = old_velocity.shape[2]
    per_row = tile_cols // BS
    tile_blocks = tile_rows // BS * per_row
    width = CYCLES * KRYLOV * (1 + SWEEPS) + 1

    is_ocean = ocean_mask.astype(jnp.float32)
    strength_part = is_ocean * ice_mask.astype(jnp.float32) * strength
    diag_tile = is_ocean * (mass_term + ocean_drag) + (1.0 - is_ocean)
    my_row = lax.axis_index("row")
    listed = ice_blocks[0]
    wanted = my_row * tile_blocks + jnp.arange(tile_blocks, dtype=jnp.int32)
    flags = jnp.any(listed[:, None] == wanted[None, :], axis=0).astype(jnp.float32)
    live_tile = jnp.repeat(
        jnp.repeat(flags.reshape(tile_rows // BS, per_row), BS, axis=0), BS, axis=1
    )
    rhs_tile = live_tile * is_ocean * (surface_stress + mass_term * old_velocity)
    fields = jnp.concatenate(
        [
            old_velocity,
            rhs_tile,
            jnp.stack([diag_tile, strength_part, live_tile, jnp.ones_like(diag_tile)]),
        ],
        axis=0,
    )
    grown = widened(fields, width)
    rhs = grown[2:4]
    diag_field = grown[4]
    live = grown[6]
    on_grid = grown[7] > 0.5

    padded = jnp.pad(grown[0:2], ((0, 0), (1, 1), (1, 1)))
    flow_u = padded[0]
    flow_v = padded[1]
    strain_xx = 0.5 * (flow_u[2:, 1:-1] - flow_u[:-2, 1:-1])
    strain_yy = 0.5 * (flow_v[1:-1, 2:] - flow_v[1:-1, :-2])
    strain_xy = 0.25 * (flow_u[1:-1, 2:] - flow_u[1:-1, :-2] + flow_v[2:, 1:-1] - flow_v[:-2, 1:-1])
    deform_sq = (
        1.25 * (strain_xx * strain_xx + strain_yy * strain_yy)
        + strain_xy * strain_xy
        + 1.5 * strain_xx * strain_yy
    )
    zeta_field = grown[5] / (2.0 * jnp.sqrt(deform_sq + DMIN_SQ))
    diagonal_total = jnp.where(on_grid, diag_field + 3.0 * zeta_field, 1.0)

    def apply_system(vector):
        return live * stencil(jnp.pad(vector, ((0, 0), (1, 1), (1, 1))), zeta_field, diag_field)

    def apply_precond(vector):
        return precondition(vector, zeta_field, diag_field, diagonal_total, width)

    def own(vector):
        return vector[:, width : width + tile_rows, width : width + tile_cols]

    def step(vector, unused):
        direction = apply_precond(vector)
        image = apply_system(direction) - SHIFT * vector
        return image, (direction, image)

    steps = CYCLES * KRYLOV
    unused, (directions, images) = lax.scan(step, rhs, None, length=steps)
    total = reduce_all(local_gram(rhs, images, width, tile_rows, tile_cols))
    update = solve_small(total, steps + 1)
    solution = update[0] * own(directions[0])
    for i in range(1, steps):
        solution = solution + update[i] * own(directions[i])
    return solution


def solution(mesh):
    return jax.shard_map(
        shards,
        mesh=mesh,
        in_specs=(
            P(None, "row", COLS),
            P(None, "row", COLS),
            P("row", COLS),
            P("row", COLS),
            P("row", COLS),
            P("row", COLS),
            P("row", COLS),
            P(COLS, None),
        ),
        out_specs=P(None, "row", COLS),
        check_vma=False,
    )
```

```python
import jax
import jax.numpy as jnp
from jax import lax
from jax.experimental import pallas as pl
from jax.experimental.pallas import tpu as pltpu
from jax.sharding import PartitionSpec as P

BS = 128
KRYLOV = 2
CYCLES = 2
SWEEPS = 2


RELAX = 0.8
DMIN_SQ = 0.25
SHIFT = 1.0

COLS = ("chip", "grp")


def combine(center, second_x, second_y, mixed, zeta_field, diag_field):
    weight_x = jnp.array([1.25, 0.25], jnp.float32)[:, None, None]
    weight_y = jnp.array([0.25, 1.25], jnp.float32)[:, None, None]
    return (
        diag_field * center
        - weight_x * zeta_field * second_x
        - weight_y * zeta_field * second_y
        - zeta_field * mixed[::-1]
    )


def stencil(padded, zeta_field, diag_field):
    center = padded[..., 1:-1, 1:-1]
    second_x = padded[..., 2:, 1:-1] + padded[..., :-2, 1:-1] - 2.0 * center
    second_y = padded[..., 1:-1, 2:] + padded[..., 1:-1, :-2] - 2.0 * center
    mixed = 0.25 * (
        padded[..., 2:, 2:] - padded[..., 2:, :-2] - padded[..., :-2, 2:] + padded[..., :-2, :-2]
    )
    return combine(center, second_x, second_y, mixed, zeta_field, diag_field)


def block_stencil(field, zeta_field, diag_field, offset):
    rows = (lax.broadcasted_iota(jnp.int32, field.shape[-2:], 0) - offset) % BS
    cols = (lax.broadcasted_iota(jnp.int32, field.shape[-2:], 1) - offset) % BS
    padded = jnp.pad(field, ((0, 0), (1, 1), (1, 1)))
    height, width = field.shape[-2:]

    def neighbour(di, dj):
        inside = jnp.ones(field.shape[-2:], jnp.bool_)
        if di:
            inside = inside & (rows != (BS - 1 if di > 0 else 0))
        if dj:
            inside = inside & (cols != (BS - 1 if dj > 0 else 0))
        window = padded[:, 1 + di : 1 + di + height, 1 + dj : 1 + dj + width]
        return jnp.where(inside, window, 0.0)

    center = field
    second_x = neighbour(1, 0) + neighbour(-1, 0) - 2.0 * center
    second_y = neighbour(0, 1) + neighbour(0, -1) - 2.0 * center
    mixed = 0.25 * (neighbour(1, 1) - neighbour(1, -1) - neighbour(-1, 1) + neighbour(-1, -1))
    return combine(center, second_x, second_y, mixed, zeta_field, diag_field)


def precondition(vector, zeta_field, diag_field, inverse_total, offset):
    iterate = vector * inverse_total
    for relaxation in range(SWEEPS):
        iterate = (
            iterate
            + RELAX
            * (vector - block_stencil(iterate, zeta_field, diag_field, offset))
            * inverse_total
        )
    return iterate


def widened(array, width):
    for axis, dim in (("row", 1), (COLS, 2)):
        size, length = (lax.axis_size(axis), array.shape[dim])
        up = [(i, i + 1) for i in range(size - 1)]
        down = [(j, i) for i, j in up]
        last = lax.slice_in_dim(array, length - width, length, axis=dim)
        initial = lax.slice_in_dim(array, 0, width, axis=dim)
        before = lax.ppermute(last, axis, up)
        after = lax.ppermute(initial, axis, down)
        array = jnp.concatenate([before, array, after], axis=dim)
    return array


def least_squares(h, start_norm):
    steps_count = KRYLOV
    row_list = [[h[i][j] for j in range(steps_count)] for i in range(steps_count + 1)]
    target_vec = [start_norm] + [jnp.zeros_like(start_norm) for i in range(steps_count)]
    for j in range(steps_count):
        upper = row_list[j][j]
        lower = row_list[j + 1][j]
        radius = jnp.sqrt(upper * upper + lower * lower)
        cosine = upper / radius
        sine_part = lower / radius
        first_row = [cosine * p + sine_part * q for p, q in zip(row_list[j], row_list[j + 1])]
        second_row = [-sine_part * p + cosine * q for p, q in zip(row_list[j], row_list[j + 1])]
        row_list[j], row_list[j + 1] = (first_row, second_row)
        first_val = cosine * target_vec[j] + sine_part * target_vec[j + 1]
        second_val = -sine_part * target_vec[j] + cosine * target_vec[j + 1]
        target_vec[j], target_vec[j + 1] = (first_val, second_val)
    weights_out = [None] * steps_count
    for j in range(steps_count - 1, -1, -1):
        accum = target_vec[j]
        for i in range(j + 1, steps_count):
            accum = accum - row_list[j][i] * weights_out[i]
        weights_out[j] = accum / row_list[j][j]
    return weights_out


def krylov_coefficients(gram):
    count = len(gram)

    def dot(p, q):
        total = None
        for i in range(count):
            for j in range(count):
                term = p[i] * gram[i][j] * q[j]
                total = term if total is None else total + term
        return total

    def shift(p):
        return [SHIFT * p[0]] + [x + SHIFT * y for x, y in zip(p[:-1], p[1:])]

    def scale(p, s):
        return [x * s for x in p]

    def axpy(p, s, q):
        return [x - s * y for x, y in zip(p, q)]

    one = jnp.ones_like(gram[0][0])
    zero = jnp.zeros_like(gram[0][0])
    residual = [one] + [zero] * (count - 1)
    solution = [zero] * count
    for restart in range(CYCLES):
        start_norm = jnp.sqrt(dot(residual, residual))
        basis_list = [scale(residual, 1.0 / start_norm)]
        images_list = []
        h = [[zero] * KRYLOV for _ in range(KRYLOV + 1)]
        for arnoldi in range(KRYLOV):
            images = shift(basis_list[arnoldi])
            images_list.append(images)
            products = [dot(images, vector) for vector in basis_list]
            for i in range(arnoldi + 1):
                images = axpy(images, products[i], basis_list[i])
            new_norm = jnp.sqrt(dot(images, images))
            for i in range(arnoldi + 1):
                h[i][arnoldi] = products[i]
            h[arnoldi + 1][arnoldi] = new_norm
            if arnoldi + 1 < KRYLOV:
                basis_list.append(scale(images, 1.0 / new_norm))
        weights_out = least_squares(h, start_norm)
        for arnoldi in range(KRYLOV):
            solution = [u + weights_out[arnoldi] * b for u, b in zip(solution, basis_list[arnoldi])]
            residual = axpy(residual, weights_out[arnoldi], images_list[arnoldi])
    return solution


def gram_kernel(count, width, tile_rows, tile_cols, *refs):
    vectors = [refs[i][...] for i in range(count)]
    out_ref = refs[count]
    extent = vectors[0].shape[-2:]
    cell_rows = lax.broadcasted_iota(jnp.int32, extent, 0)
    cell_cols = lax.broadcasted_iota(jnp.int32, extent, 1)
    own = (
        (cell_rows >= width)
        & (cell_rows < width + tile_rows)
        & (cell_cols >= width)
        & (cell_cols < width + tile_cols)
    )
    vectors = [jnp.where(own, v, 0.0) for v in vectors]
    shape = out_ref.shape
    rows = lax.broadcasted_iota(jnp.int32, shape, 0)
    lanes = lax.broadcasted_iota(jnp.int32, shape, 1)
    result = jnp.zeros(shape, jnp.float32)
    index = 0
    for i in range(count):
        for j in range(i, count):
            product = jnp.sum(vectors[i] * vectors[j], axis=0)
            part = jnp.sum(jnp.sum(product, axis=0, keepdims=True), axis=1, keepdims=True)
            result = jnp.where((rows == 0) & (lanes == index), part, result)
            index += 1
    out_ref[...] = result


def local_gram(krylov, width, tile_rows, tile_cols):
    count = len(krylov)
    return pl.pallas_call(
        lambda *refs: gram_kernel(count, width, tile_rows, tile_cols, *refs),
        out_shape=jax.ShapeDtypeStruct((8, 128), jnp.float32),
        in_specs=[pl.BlockSpec(memory_space=pltpu.VMEM)] * count,
        out_specs=pl.BlockSpec(memory_space=pltpu.VMEM),
    )(*krylov)


def coefficients_kernel(count, total_ref, out_ref):
    shape = out_ref.shape
    pairs = [(i, j) for i in range(count) for j in range(i, count)]
    gram = [[None] * count for _ in range(count)]
    for index, (i, j) in enumerate(pairs):
        value = jnp.full(shape, total_ref[0, index], jnp.float32)
        gram[i][j] = value
        gram[j][i] = value
    update = krylov_coefficients(gram)
    rows = lax.broadcasted_iota(jnp.int32, shape, 0)
    result = jnp.zeros(shape, jnp.float32)
    for k, value in enumerate(update[: count - 1]):
        result = jnp.where(rows == k, value, result)
    out_ref[...] = result


def solve_small(total, count):
    out = pl.pallas_call(
        lambda total_ref, out_ref: coefficients_kernel(count, total_ref, out_ref),
        out_shape=jax.ShapeDtypeStruct((8, 128), jnp.float32),
        in_specs=[pl.BlockSpec(memory_space=pltpu.SMEM)],
        out_specs=pl.BlockSpec(memory_space=pltpu.VMEM),
    )(total)
    column = out[:, 0]
    return [column[k] for k in range(count - 1)]


def butterfly(values, axis):
    size = lax.axis_size(axis)
    stride = 1
    while stride < size:
        values = values + lax.ppermute(values, axis, [(i, i ^ stride) for i in range(size)])
        stride *= 2
    return values


def reduce_all(values):
    return butterfly(butterfly(butterfly(values, "chip"), "row"), "grp")


def shards(
    old_velocity, surface_stress, mass_term, ocean_drag, strength, ice_mask, ocean_mask, ice_blocks
):
    tile_rows = old_velocity.shape[1]
    tile_cols = old_velocity.shape[2]
    per_row = tile_cols // BS
    tile_blocks = tile_rows // BS * per_row
    width = CYCLES * KRYLOV * (1 + SWEEPS) + 1

    is_ocean = ocean_mask.astype(jnp.float32)
    strength_part = is_ocean * ice_mask.astype(jnp.float32) * strength
    diag_tile = is_ocean * (mass_term + ocean_drag) + (1.0 - is_ocean)
    my_row = lax.axis_index("row")
    listed = ice_blocks[0]
    wanted = my_row * tile_blocks + jnp.arange(tile_blocks, dtype=jnp.int32)
    flags = jnp.any(listed[:, None] == wanted[None, :], axis=0).astype(jnp.float32)
    live_tile = jnp.repeat(
        jnp.repeat(flags.reshape(tile_rows // BS, per_row), BS, axis=0), BS, axis=1
    )
    rhs_tile = live_tile * is_ocean * (surface_stress + mass_term * old_velocity)
    fields = jnp.concatenate(
        [
            old_velocity,
            rhs_tile,
            jnp.stack([diag_tile, strength_part, live_tile]),
        ],
        axis=0,
    )
    grown = widened(fields, width)
    rhs = grown[2:4]
    diag_field = grown[4]
    live = grown[6]
    on_grid = diag_field > 0.0

    padded = jnp.pad(grown[0:2], ((0, 0), (1, 1), (1, 1)))
    flow_u = padded[0]
    flow_v = padded[1]
    strain_xx = 0.5 * (flow_u[2:, 1:-1] - flow_u[:-2, 1:-1])
    strain_yy = 0.5 * (flow_v[1:-1, 2:] - flow_v[1:-1, :-2])
    strain_xy = 0.25 * (flow_u[1:-1, 2:] - flow_u[1:-1, :-2] + flow_v[2:, 1:-1] - flow_v[:-2, 1:-1])
    deform_sq = (
        1.25 * (strain_xx * strain_xx + strain_yy * strain_yy)
        + strain_xy * strain_xy
        + 1.5 * strain_xx * strain_yy
    )
    zeta_field = grown[5] / (2.0 * jnp.sqrt(deform_sq + DMIN_SQ))
    inverse_total = 1.0 / jnp.where(on_grid, diag_field + 3.0 * zeta_field, 1.0)

    def apply_system(vector):
        return live * stencil(jnp.pad(vector, ((0, 0), (1, 1), (1, 1))), zeta_field, diag_field)

    def apply_precond(vector):
        return precondition(vector, zeta_field, diag_field, inverse_total, width)

    def own(vector):
        return vector[:, width : width + tile_rows, width : width + tile_cols]

    krylov = [rhs]
    directions = []
    for step in range(CYCLES * KRYLOV):
        directions.append(apply_precond(krylov[-1]))
        krylov.append(apply_system(directions[-1]) - SHIFT * krylov[-1])
    total = reduce_all(local_gram(krylov, width, tile_rows, tile_cols))
    update = solve_small(total, len(krylov))
    solution = update[0] * own(directions[0])
    for i in range(1, len(directions)):
        solution = solution + update[i] * own(directions[i])
    return solution


def solution(mesh):
    return jax.shard_map(
        shards,
        mesh=mesh,
        in_specs=(
            P(None, "row", COLS),
            P(None, "row", COLS),
            P("row", COLS),
            P("row", COLS),
            P("row", COLS),
            P("row", COLS),
            P("row", COLS),
            P(COLS, None),
        ),
        out_specs=P(None, "row", COLS),
        check_vma=False,
    )
```

```python
import jax
import jax.numpy as jnp
from jax import lax
from jax.experimental import pallas as pl
from jax.experimental.pallas import tpu as pltpu
from jax.sharding import PartitionSpec as P

BS = 128
KRYLOV = 2
CYCLES = 2
SWEEPS = 2


RELAX = 0.8
DMIN_SQ = 0.25
SHIFT = 1.0

COLS = ("chip", "grp")


def combine(center, second_x, second_y, mixed, zeta_field, diag_field):
    weight_x = jnp.array([1.25, 0.25], jnp.float32)[:, None, None]
    weight_y = jnp.array([0.25, 1.25], jnp.float32)[:, None, None]
    return (
        diag_field * center
        - weight_x * zeta_field * second_x
        - weight_y * zeta_field * second_y
        - zeta_field * mixed[::-1]
    )


def stencil(padded, zeta_field, diag_field):
    center = padded[..., 1:-1, 1:-1]
    second_x = padded[..., 2:, 1:-1] + padded[..., :-2, 1:-1] - 2.0 * center
    second_y = padded[..., 1:-1, 2:] + padded[..., 1:-1, :-2] - 2.0 * center
    mixed = 0.25 * (
        padded[..., 2:, 2:] - padded[..., 2:, :-2] - padded[..., :-2, 2:] + padded[..., :-2, :-2]
    )
    return combine(center, second_x, second_y, mixed, zeta_field, diag_field)


def block_stencil(field, zeta_field, diag_field, offset):
    rows = (lax.broadcasted_iota(jnp.int32, field.shape[-2:], 0) - offset) % BS
    cols = (lax.broadcasted_iota(jnp.int32, field.shape[-2:], 1) - offset) % BS
    padded = jnp.pad(field, ((0, 0), (1, 1), (1, 1)))
    height, width = field.shape[-2:]

    def neighbour(di, dj):
        inside = jnp.ones(field.shape[-2:], jnp.bool_)
        if di:
            inside = inside & (rows != (BS - 1 if di > 0 else 0))
        if dj:
            inside = inside & (cols != (BS - 1 if dj > 0 else 0))
        window = padded[:, 1 + di : 1 + di + height, 1 + dj : 1 + dj + width]
        return jnp.where(inside, window, 0.0)

    center = field
    second_x = neighbour(1, 0) + neighbour(-1, 0) - 2.0 * center
    second_y = neighbour(0, 1) + neighbour(0, -1) - 2.0 * center
    mixed = 0.25 * (neighbour(1, 1) - neighbour(1, -1) - neighbour(-1, 1) + neighbour(-1, -1))
    return combine(center, second_x, second_y, mixed, zeta_field, diag_field)


def precondition(vector, zeta_field, diag_field, inverse_total, offset):
    iterate = vector * inverse_total
    for relaxation in range(SWEEPS):
        iterate = (
            iterate
            + RELAX
            * (vector - block_stencil(iterate, zeta_field, diag_field, offset))
            * inverse_total
        )
    return iterate


def widened(array, width):
    for axis, dim in (("row", 1), (COLS, 2)):
        size, length = (lax.axis_size(axis), array.shape[dim])
        up = [(i, i + 1) for i in range(size - 1)]
        down = [(j, i) for i, j in up]
        last = lax.slice_in_dim(array, length - width, length, axis=dim)
        initial = lax.slice_in_dim(array, 0, width, axis=dim)
        before = lax.ppermute(last, axis, up)
        after = lax.ppermute(initial, axis, down)
        array = jnp.concatenate([before, array, after], axis=dim)
    return array


def least_squares(h, start_norm):
    steps_count = KRYLOV
    row_list = [[h[i][j] for j in range(steps_count)] for i in range(steps_count + 1)]
    target_vec = [start_norm] + [jnp.zeros_like(start_norm) for i in range(steps_count)]
    for j in range(steps_count):
        upper = row_list[j][j]
        lower = row_list[j + 1][j]
        radius = jnp.sqrt(upper * upper + lower * lower)
        cosine = upper / radius
        sine_part = lower / radius
        first_row = [cosine * p + sine_part * q for p, q in zip(row_list[j], row_list[j + 1])]
        second_row = [-sine_part * p + cosine * q for p, q in zip(row_list[j], row_list[j + 1])]
        row_list[j], row_list[j + 1] = (first_row, second_row)
        first_val = cosine * target_vec[j] + sine_part * target_vec[j + 1]
        second_val = -sine_part * target_vec[j] + cosine * target_vec[j + 1]
        target_vec[j], target_vec[j + 1] = (first_val, second_val)
    weights_out = [None] * steps_count
    for j in range(steps_count - 1, -1, -1):
        accum = target_vec[j]
        for i in range(j + 1, steps_count):
            accum = accum - row_list[j][i] * weights_out[i]
        weights_out[j] = accum / row_list[j][j]
    return weights_out


def krylov_coefficients(gram):
    count = len(gram)

    def dot(p, q):
        total = None
        for i in range(count):
            for j in range(count):
                term = p[i] * gram[i][j] * q[j]
                total = term if total is None else total + term
        return total

    def shift(p):
        return [SHIFT * p[0]] + [x + SHIFT * y for x, y in zip(p[:-1], p[1:])]

    def scale(p, s):
        return [x * s for x in p]

    def axpy(p, s, q):
        return [x - s * y for x, y in zip(p, q)]

    one = jnp.ones_like(gram[0][0])
    zero = jnp.zeros_like(gram[0][0])
    residual = [one] + [zero] * (count - 1)
    solution = [zero] * count
    for restart in range(CYCLES):
        start_norm = jnp.sqrt(dot(residual, residual))
        basis_list = [scale(residual, 1.0 / start_norm)]
        images_list = []
        h = [[zero] * KRYLOV for _ in range(KRYLOV + 1)]
        for arnoldi in range(KRYLOV):
            images = shift(basis_list[arnoldi])
            images_list.append(images)
            products = [dot(images, vector) for vector in basis_list]
            for i in range(arnoldi + 1):
                images = axpy(images, products[i], basis_list[i])
            new_norm = jnp.sqrt(dot(images, images))
            for i in range(arnoldi + 1):
                h[i][arnoldi] = products[i]
            h[arnoldi + 1][arnoldi] = new_norm
            if arnoldi + 1 < KRYLOV:
                basis_list.append(scale(images, 1.0 / new_norm))
        weights_out = least_squares(h, start_norm)
        for arnoldi in range(KRYLOV):
            solution = [u + weights_out[arnoldi] * b for u, b in zip(solution, basis_list[arnoldi])]
            residual = axpy(residual, weights_out[arnoldi], images_list[arnoldi])
    return solution


def gram_kernel(count, width, tile_rows, tile_cols, *refs):
    vectors = [refs[i][...] for i in range(count)]
    out_ref = refs[count]
    extent = vectors[0].shape[-2:]
    cell_rows = lax.broadcasted_iota(jnp.int32, extent, 0)
    cell_cols = lax.broadcasted_iota(jnp.int32, extent, 1)
    own = (
        (cell_rows >= width)
        & (cell_rows < width + tile_rows)
        & (cell_cols >= width)
        & (cell_cols < width + tile_cols)
    )
    vectors = [jnp.where(own, v, 0.0) for v in vectors]
    shape = out_ref.shape
    rows = lax.broadcasted_iota(jnp.int32, shape, 0)
    lanes = lax.broadcasted_iota(jnp.int32, shape, 1)
    result = jnp.zeros(shape, jnp.float32)
    index = 0
    for i in range(count):
        for j in range(i, count):
            product = jnp.sum(vectors[i] * vectors[j], axis=0)
            part = jnp.sum(jnp.sum(product, axis=0, keepdims=True), axis=1, keepdims=True)
            result = jnp.where((rows == 0) & (lanes == index), part, result)
            index += 1
    out_ref[...] = result


def local_gram(krylov, width, tile_rows, tile_cols):
    count = len(krylov)
    return pl.pallas_call(
        lambda *refs: gram_kernel(count, width, tile_rows, tile_cols, *refs),
        out_shape=jax.ShapeDtypeStruct((8, 128), jnp.float32),
        in_specs=[pl.BlockSpec(memory_space=pltpu.VMEM)] * count,
        out_specs=pl.BlockSpec(memory_space=pltpu.VMEM),
    )(*krylov)


def coefficients_kernel(count, total_ref, *refs):
    direction_refs, out_ref = refs[:-1], refs[-1]
    shape = (8, 128)
    pairs = [(i, j) for i in range(count) for j in range(i, count)]
    gram = [[None] * count for _ in range(count)]
    for index, (i, j) in enumerate(pairs):
        value = jnp.full(shape, total_ref[0, index], jnp.float32)
        gram[i][j] = value
        gram[j][i] = value
    update = krylov_coefficients(gram)
    solution = None
    for k, direction_ref in enumerate(direction_refs):
        term = update[k][0:1, 0:1] * direction_ref[...]
        solution = term if solution is None else solution + term
    out_ref[...] = solution


def solve_small(total, directions):
    count = len(directions) + 1
    return pl.pallas_call(
        lambda total_ref, *refs: coefficients_kernel(count, total_ref, *refs),
        out_shape=jax.ShapeDtypeStruct(directions[0].shape, jnp.float32),
        in_specs=[pl.BlockSpec(memory_space=pltpu.SMEM)]
        + [pl.BlockSpec(memory_space=pltpu.VMEM)] * len(directions),
        out_specs=pl.BlockSpec(memory_space=pltpu.VMEM),
    )(total, *directions)


def butterfly(values, axis):
    size = lax.axis_size(axis)
    stride = 1
    while stride < size:
        values = values + lax.ppermute(values, axis, [(i, i ^ stride) for i in range(size)])
        stride *= 2
    return values


def reduce_all(values):
    return butterfly(butterfly(butterfly(values, "chip"), "row"), "grp")


def shards(
    old_velocity, surface_stress, mass_term, ocean_drag, strength, ice_mask, ocean_mask, ice_blocks
):
    tile_rows = old_velocity.shape[1]
    tile_cols = old_velocity.shape[2]
    per_row = tile_cols // BS
    tile_blocks = tile_rows // BS * per_row
    width = CYCLES * KRYLOV * (1 + SWEEPS) + 1

    is_ocean = ocean_mask.astype(jnp.float32)
    strength_part = is_ocean * ice_mask.astype(jnp.float32) * strength
    diag_tile = is_ocean * (mass_term + ocean_drag) + (1.0 - is_ocean)
    my_row = lax.axis_index("row")
    listed = ice_blocks[0]
    wanted = my_row * tile_blocks + jnp.arange(tile_blocks, dtype=jnp.int32)
    flags = jnp.any(listed[:, None] == wanted[None, :], axis=0).astype(jnp.float32)
    live_tile = jnp.repeat(
        jnp.repeat(flags.reshape(tile_rows // BS, per_row), BS, axis=0), BS, axis=1
    )
    rhs_tile = live_tile * is_ocean * (surface_stress + mass_term * old_velocity)
    fields = jnp.concatenate(
        [
            old_velocity,
            rhs_tile,
            jnp.stack([diag_tile, strength_part, live_tile]),
        ],
        axis=0,
    )
    grown = widened(fields, width)
    rhs = grown[2:4]
    diag_field = grown[4]
    live = grown[6]
    on_grid = diag_field > 0.0

    padded = jnp.pad(grown[0:2], ((0, 0), (1, 1), (1, 1)))
    flow_u = padded[0]
    flow_v = padded[1]
    strain_xx = 0.5 * (flow_u[2:, 1:-1] - flow_u[:-2, 1:-1])
    strain_yy = 0.5 * (flow_v[1:-1, 2:] - flow_v[1:-1, :-2])
    strain_xy = 0.25 * (flow_u[1:-1, 2:] - flow_u[1:-1, :-2] + flow_v[2:, 1:-1] - flow_v[:-2, 1:-1])
    deform_sq = (
        1.25 * (strain_xx * strain_xx + strain_yy * strain_yy)
        + strain_xy * strain_xy
        + 1.5 * strain_xx * strain_yy
    )
    zeta_field = grown[5] / (2.0 * jnp.sqrt(deform_sq + DMIN_SQ))
    inverse_total = 1.0 / jnp.where(on_grid, diag_field + 3.0 * zeta_field, 1.0)

    def apply_system(vector):
        return live * stencil(jnp.pad(vector, ((0, 0), (1, 1), (1, 1))), zeta_field, diag_field)

    def apply_precond(vector):
        return precondition(vector, zeta_field, diag_field, inverse_total, width)

    def own(vector):
        return vector[:, width : width + tile_rows, width : width + tile_cols]

    krylov = [rhs]
    directions = []
    for step in range(CYCLES * KRYLOV):
        directions.append(apply_precond(krylov[-1]))
        krylov.append(apply_system(directions[-1]) - SHIFT * krylov[-1])
    total = reduce_all(local_gram(krylov, width, tile_rows, tile_cols))
    solution = own(solve_small(total, directions))
    return solution


def solution(mesh):
    return jax.shard_map(
        shards,
        mesh=mesh,
        in_specs=(
            P(None, "row", COLS),
            P(None, "row", COLS),
            P("row", COLS),
            P("row", COLS),
            P("row", COLS),
            P("row", COLS),
            P("row", COLS),
            P(COLS, None),
        ),
        out_specs=P(None, "row", COLS),
        check_vma=False,
    )
```

```python
import jax
import jax.numpy as jnp
from jax import lax
from jax.experimental import pallas as pl
from jax.experimental.pallas import tpu as pltpu
from jax.sharding import PartitionSpec as P

BS = 128
KRYLOV = 2
CYCLES = 2
SWEEPS = 2


RELAX = 0.8
DMIN_SQ = 0.25
SHIFT = 1.0

COLS = ("chip", "grp")


def combine(center, second_x, second_y, mixed, zeta_field, diag_field):
    weight_x = jnp.array([1.25, 0.25], jnp.float32)[:, None, None]
    weight_y = jnp.array([0.25, 1.25], jnp.float32)[:, None, None]
    return (
        diag_field * center
        - weight_x * zeta_field * second_x
        - weight_y * zeta_field * second_y
        - zeta_field * mixed[::-1]
    )


def stencil(padded, zeta_field, diag_field):
    center = padded[..., 1:-1, 1:-1]
    second_x = padded[..., 2:, 1:-1] + padded[..., :-2, 1:-1] - 2.0 * center
    second_y = padded[..., 1:-1, 2:] + padded[..., 1:-1, :-2] - 2.0 * center
    mixed = 0.25 * (
        padded[..., 2:, 2:] - padded[..., 2:, :-2] - padded[..., :-2, 2:] + padded[..., :-2, :-2]
    )
    return combine(center, second_x, second_y, mixed, zeta_field, diag_field)


def block_stencil(field, zeta_field, diag_field, offset):
    rows = (lax.broadcasted_iota(jnp.int32, field.shape[-2:], 0) - offset) % BS
    cols = (lax.broadcasted_iota(jnp.int32, field.shape[-2:], 1) - offset) % BS
    padded = jnp.pad(field, ((0, 0), (1, 1), (1, 1)))
    height, width = field.shape[-2:]

    def neighbour(di, dj):
        inside = jnp.ones(field.shape[-2:], jnp.bool_)
        if di:
            inside = inside & (rows != (BS - 1 if di > 0 else 0))
        if dj:
            inside = inside & (cols != (BS - 1 if dj > 0 else 0))
        window = padded[:, 1 + di : 1 + di + height, 1 + dj : 1 + dj + width]
        return jnp.where(inside, window, 0.0)

    center = field
    second_x = neighbour(1, 0) + neighbour(-1, 0) - 2.0 * center
    second_y = neighbour(0, 1) + neighbour(0, -1) - 2.0 * center
    mixed = 0.25 * (neighbour(1, 1) - neighbour(1, -1) - neighbour(-1, 1) + neighbour(-1, -1))
    return combine(center, second_x, second_y, mixed, zeta_field, diag_field)


def precondition(vector, zeta_field, diag_field, inverse_total, offset):
    iterate = vector * inverse_total
    for relaxation in range(SWEEPS):
        iterate = (
            iterate
            + RELAX
            * (vector - block_stencil(iterate, zeta_field, diag_field, offset))
            * inverse_total
        )
    return iterate


def widened(array, width):
    for axis, dim in (("row", 1), (COLS, 2)):
        size, length = (lax.axis_size(axis), array.shape[dim])
        up = [(i, i + 1) for i in range(size - 1)]
        down = [(j, i) for i, j in up]
        last = lax.slice_in_dim(array, length - width, length, axis=dim)
        initial = lax.slice_in_dim(array, 0, width, axis=dim)
        before = lax.ppermute(last, axis, up)
        after = lax.ppermute(initial, axis, down)
        array = jnp.concatenate([before, array, after], axis=dim)
    return array


def least_squares(h, start_norm):
    steps_count = KRYLOV
    row_list = [[h[i][j] for j in range(steps_count)] for i in range(steps_count + 1)]
    target_vec = [start_norm] + [jnp.zeros_like(start_norm) for i in range(steps_count)]
    for j in range(steps_count):
        upper = row_list[j][j]
        lower = row_list[j + 1][j]
        radius = jnp.sqrt(upper * upper + lower * lower)
        cosine = upper / radius
        sine_part = lower / radius
        first_row = [cosine * p + sine_part * q for p, q in zip(row_list[j], row_list[j + 1])]
        second_row = [-sine_part * p + cosine * q for p, q in zip(row_list[j], row_list[j + 1])]
        row_list[j], row_list[j + 1] = (first_row, second_row)
        first_val = cosine * target_vec[j] + sine_part * target_vec[j + 1]
        second_val = -sine_part * target_vec[j] + cosine * target_vec[j + 1]
        target_vec[j], target_vec[j + 1] = (first_val, second_val)
    weights_out = [None] * steps_count
    for j in range(steps_count - 1, -1, -1):
        accum = target_vec[j]
        for i in range(j + 1, steps_count):
            accum = accum - row_list[j][i] * weights_out[i]
        weights_out[j] = accum / row_list[j][j]
    return weights_out


def krylov_coefficients(gram):
    count = len(gram)

    def dot(p, q):
        total = None
        for i in range(count):
            for j in range(count):
                term = p[i] * gram[i][j] * q[j]
                total = term if total is None else total + term
        return total

    def shift(p):
        return [SHIFT * p[0]] + [x + SHIFT * y for x, y in zip(p[:-1], p[1:])]

    def scale(p, s):
        return [x * s for x in p]

    def axpy(p, s, q):
        return [x - s * y for x, y in zip(p, q)]

    one = jnp.ones_like(gram[0][0])
    zero = jnp.zeros_like(gram[0][0])
    residual = [one] + [zero] * (count - 1)
    solution = [zero] * count
    for restart in range(CYCLES):
        start_norm = jnp.sqrt(dot(residual, residual))
        basis_list = [scale(residual, 1.0 / start_norm)]
        images_list = []
        h = [[zero] * KRYLOV for _ in range(KRYLOV + 1)]
        for arnoldi in range(KRYLOV):
            images = shift(basis_list[arnoldi])
            images_list.append(images)
            products = [dot(images, vector) for vector in basis_list]
            for i in range(arnoldi + 1):
                images = axpy(images, products[i], basis_list[i])
            new_norm = jnp.sqrt(dot(images, images))
            for i in range(arnoldi + 1):
                h[i][arnoldi] = products[i]
            h[arnoldi + 1][arnoldi] = new_norm
            if arnoldi + 1 < KRYLOV:
                basis_list.append(scale(images, 1.0 / new_norm))
        weights_out = least_squares(h, start_norm)
        for arnoldi in range(KRYLOV):
            solution = [u + weights_out[arnoldi] * b for u, b in zip(solution, basis_list[arnoldi])]
            residual = axpy(residual, weights_out[arnoldi], images_list[arnoldi])
    return solution


def gram_kernel(count, width, tile_rows, tile_cols, *refs):
    low = width // 8 * 8
    high = (width + tile_rows + 7) // 8 * 8
    vectors = [refs[i][:, low:high, :] for i in range(count)]
    out_ref = refs[count]
    extent = vectors[0].shape[-2:]
    cell_rows = lax.broadcasted_iota(jnp.int32, extent, 0) + low
    cell_cols = lax.broadcasted_iota(jnp.int32, extent, 1)
    own = (
        (cell_rows >= width)
        & (cell_rows < width + tile_rows)
        & (cell_cols >= width)
        & (cell_cols < width + tile_cols)
    )
    vectors = [jnp.where(own, v, 0.0) for v in vectors]
    shape = out_ref.shape
    rows = lax.broadcasted_iota(jnp.int32, shape, 0)
    lanes = lax.broadcasted_iota(jnp.int32, shape, 1)
    result = jnp.zeros(shape, jnp.float32)
    index = 0
    for i in range(count):
        for j in range(i, count):
            product = jnp.sum(vectors[i] * vectors[j], axis=0)
            part = jnp.sum(jnp.sum(product, axis=0, keepdims=True), axis=1, keepdims=True)
            result = jnp.where((rows == 0) & (lanes == index), part, result)
            index += 1
    out_ref[...] = result


def local_gram(krylov, width, tile_rows, tile_cols):
    count = len(krylov)
    return pl.pallas_call(
        lambda *refs: gram_kernel(count, width, tile_rows, tile_cols, *refs),
        out_shape=jax.ShapeDtypeStruct((8, 128), jnp.float32),
        in_specs=[pl.BlockSpec(memory_space=pltpu.VMEM)] * count,
        out_specs=pl.BlockSpec(memory_space=pltpu.VMEM),
    )(*krylov)


def coefficients_kernel(count, total_ref, *refs):
    direction_refs, out_ref = refs[:-1], refs[-1]
    shape = (8, 128)
    pairs = [(i, j) for i in range(count) for j in range(i, count)]
    gram = [[None] * count for _ in range(count)]
    for index, (i, j) in enumerate(pairs):
        value = jnp.full(shape, total_ref[0, index], jnp.float32)
        gram[i][j] = value
        gram[j][i] = value
    update = krylov_coefficients(gram)
    solution = None
    for k, direction_ref in enumerate(direction_refs):
        term = update[k][0:1, 0:1] * direction_ref[...]
        solution = term if solution is None else solution + term
    out_ref[...] = solution


def solve_small(total, directions):
    count = len(directions) + 1
    return pl.pallas_call(
        lambda total_ref, *refs: coefficients_kernel(count, total_ref, *refs),
        out_shape=jax.ShapeDtypeStruct(directions[0].shape, jnp.float32),
        in_specs=[pl.BlockSpec(memory_space=pltpu.SMEM)]
        + [pl.BlockSpec(memory_space=pltpu.VMEM)] * len(directions),
        out_specs=pl.BlockSpec(memory_space=pltpu.VMEM),
    )(total, *directions)


def butterfly(values, axis):
    size = lax.axis_size(axis)
    stride = 1
    while stride < size:
        values = values + lax.ppermute(values, axis, [(i, i ^ stride) for i in range(size)])
        stride *= 2
    return values


def reduce_all(values):
    return butterfly(butterfly(butterfly(values, "chip"), "row"), "grp")


def shards(
    old_velocity, surface_stress, mass_term, ocean_drag, strength, ice_mask, ocean_mask, ice_blocks
):
    tile_rows = old_velocity.shape[1]
    tile_cols = old_velocity.shape[2]
    per_row = tile_cols // BS
    tile_blocks = tile_rows // BS * per_row
    width = CYCLES * KRYLOV * (1 + SWEEPS) + 1

    is_ocean = ocean_mask.astype(jnp.float32)
    strength_part = is_ocean * ice_mask.astype(jnp.float32) * strength
    diag_tile = is_ocean * (mass_term + ocean_drag) + (1.0 - is_ocean)
    my_row = lax.axis_index("row")
    listed = ice_blocks[0]
    wanted = my_row * tile_blocks + jnp.arange(tile_blocks, dtype=jnp.int32)
    flags = jnp.any(listed[:, None] == wanted[None, :], axis=0).astype(jnp.float32)
    live_tile = jnp.repeat(
        jnp.repeat(flags.reshape(tile_rows // BS, per_row), BS, axis=0), BS, axis=1
    )
    rhs_tile = live_tile * is_ocean * (surface_stress + mass_term * old_velocity)
    fields = jnp.concatenate(
        [
            old_velocity,
            rhs_tile,
            jnp.stack([diag_tile, strength_part, live_tile]),
        ],
        axis=0,
    )
    grown = widened(fields, width)
    rhs = grown[2:4]
    diag_field = grown[4]
    live = grown[6]
    on_grid = diag_field > 0.0

    padded = jnp.pad(grown[0:2], ((0, 0), (1, 1), (1, 1)))
    flow_u = padded[0]
    flow_v = padded[1]
    strain_xx = 0.5 * (flow_u[2:, 1:-1] - flow_u[:-2, 1:-1])
    strain_yy = 0.5 * (flow_v[1:-1, 2:] - flow_v[1:-1, :-2])
    strain_xy = 0.25 * (flow_u[1:-1, 2:] - flow_u[1:-1, :-2] + flow_v[2:, 1:-1] - flow_v[:-2, 1:-1])
    deform_sq = (
        1.25 * (strain_xx * strain_xx + strain_yy * strain_yy)
        + strain_xy * strain_xy
        + 1.5 * strain_xx * strain_yy
    )
    zeta_field = grown[5] / (2.0 * jnp.sqrt(deform_sq + DMIN_SQ))
    inverse_total = 1.0 / jnp.where(on_grid, diag_field + 3.0 * zeta_field, 1.0)

    def apply_system(vector):
        return live * stencil(jnp.pad(vector, ((0, 0), (1, 1), (1, 1))), zeta_field, diag_field)

    def apply_precond(vector):
        return precondition(vector, zeta_field, diag_field, inverse_total, width)

    def own(vector):
        return vector[:, width : width + tile_rows, width : width + tile_cols]

    krylov = [rhs]
    directions = []
    for step in range(CYCLES * KRYLOV):
        directions.append(apply_precond(krylov[-1]))
        krylov.append(apply_system(directions[-1]) - SHIFT * krylov[-1])
    total = reduce_all(local_gram(krylov, width, tile_rows, tile_cols)[0:1])
    solution = own(solve_small(total, directions))
    return solution


def solution(mesh):
    return jax.shard_map(
        shards,
        mesh=mesh,
        in_specs=(
            P(None, "row", COLS),
            P(None, "row", COLS),
            P("row", COLS),
            P("row", COLS),
            P("row", COLS),
            P("row", COLS),
            P("row", COLS),
            P(COLS, None),
        ),
        out_specs=P(None, "row", COLS),
        check_vma=False,
    )
```
